32 devices in a mesh: seq: 8 (over y, x, core), head: 4 (over z).
Axes of the slice: x: 2, y: 2, z: 4, core: 2. Of those that a mesh axis runs over, the one named last changes fastest.
Arguments:
- tokens: bfloat16 [4096, 5376], P('seq', 'head'), may hold values from -32 to 32
- query_weight: bfloat16 [5376, 4096], P(None, 'head'), may hold values from -1 to 1
- key_weight: bfloat16 [5376, 2048], P(None, 'head'), may hold values from -1 to 1
- value_weight: bfloat16 [5376, 2048], P(None, 'head'), may hold values from -0.078125 to 0.078125
- output_grad: bfloat16 [4096, 4096], P('seq', 'head'), may hold values from -48 to 48
- segments: int32 [4096], replicated, may hold values from 0 to 3, never falling along the last dimension, each value on 1 to 2048 neighbouring positions
Outputs:
- token_grad: bfloat16 [4096, 5376], P('seq', 'head')
- query_weight_grad: bfloat16 [5376, 4096], P('seq', 'head')
- key_weight_grad: bfloat16 [5376, 2048], P('seq', 'head')
- value_weight_grad: bfloat16 [5376, 2048], P('seq', 'head')
The draws below stay inside these ranges and needn't reach their ends.
Inputs may be any that keep to these rules, and one draw needn't show every extreme that they name: `segments`: segment numbers never fall along the tokens; a segment has at most 2048 tokens.
All inputs are finite; a program needn't handle non-finite values.
Results may differ from the reference program's by a relative error of at most 0.015.
The reference program's roundings to bfloat16 on the way (of `queries`, `dscores`, `probs_low` and `query_grad`) count: a program that leaves them out, or rounds other values in their place, can miss the bound.
Values may be sent and summed in bfloat16 or wider, within the bound.
No kernel may reach another device: no remote copies, remote signals or barrier semaphores. Data moves between devices by JAX's collectives and lax.ppermute only.
A program may use at most 192 MiB of HBM per device.

```python
import math
import jax
import jax.numpy as jnp
import numpy as np
from jax import lax

D = 5376
HEADS = 32
KV_HEADS = 16
HEAD_DIM = 128
WINDOW = 1024
TOK_DEV = 512
HOPS = 2
TOKENS = 4096
N_HEAD = 4


def key_base(key):
    sub_key = jax.random.fold_in(key, 101)
    return jax.random.truncated_normal(sub_key, -6.0, 6.0, (D, KV_HEADS * HEAD_DIM), jnp.float32) * D ** (-0.5)


def draw_tokens(key, part):
    values = jax.random.truncated_normal(key, -6.0, 6.0, (TOKENS, D), jnp.float32)
    return values.astype(jnp.bfloat16)


def draw_key_weight(key, part):
    base = key_base(key)
    return base.astype(jnp.bfloat16)


def draw_query_weight(key, part):
    noise_key = jax.random.fold_in(key, 202)
    noise = jax.random.truncated_normal(noise_key, -6.0, 6.0, (D, HEADS * HEAD_DIM), jnp.float32) * D ** (-0.5)
    return noise.astype(jnp.bfloat16)


def block_levels(stream_key, extent, cuts, low, top_value):
    def one(dim, parts):
        draws = jax.random.uniform(jax.random.fold_in(jax.random.fold_in(stream_key, 6), dim), (parts,), jnp.float32, low / len(cuts), top_value / len(cuts))
        return jnp.repeat(jnp.exp(draws), extent[dim] // parts).reshape((-1,) + (1,) * (len(extent) - dim - 1))

    gain = one(*cuts[0])
    for cut in cuts[1:]:
        gain = gain * one(*cut)
    return gain


def length_profile(count, total, limit, skew):
    loads = [(1 << 20) // math.isqrt(rank ** skew) + 1 for rank in range(2, count + 1)]
    surplus, given = total - limit - (count - 1), [1] * (count - 1)
    while surplus > 0:
        free = [i for i in range(count - 1) if given[i] < limit]
        mass, remaining = sum([loads[i] for i in free]), surplus
        for i in free:
            more = min(limit - given[i], max(1, remaining * loads[i] // mass), surplus)
            given[i] = given[i] + more
            surplus = surplus - more
    return np.array([limit] + given)


def ragged_sizes(rng, count, total, reach, skew):
    if count == 2:
        one = jax.random.randint(rng, (), max(1, total - reach), min(reach, total - 1) + 1)
        return jnp.stack([one, total - one])
    tallies = jnp.asarray(length_profile(count, total, reach, skew), jnp.int32)
    twos = (count - 1) // 2
    source_of, taker = tallies[1:1 + 2 * twos:2], tallies[2:2 + 2 * twos:2]
    room = jnp.minimum(source_of - 1, reach - taker)
    moved = jax.random.randint(jax.random.fold_in(rng, 1), (twos,), 0, 1 << 20) % (room + 1)
    tallies = tallies.at[1:1 + 2 * twos:2].set(source_of - moved).at[2:2 + 2 * twos:2].set(taker + moved)
    return tallies[jax.random.permutation(jax.random.fold_in(rng, 2), count)]


def centred(own_key, dims, deviation, most, pieces=(), held_as=jnp.bfloat16):
    result = deviation * jax.random.normal(own_key, dims, jnp.float32)
    if pieces:
        result = result * block_levels(own_key, dims, pieces, -0.22, 0.18)
    return jnp.clip(result, -most, most).astype(held_as)


def setup_inputs(seed: int = 0) -> dict:
    key_list = jax.random.split(jax.random.key(seed), 7)
    tokens = draw_tokens(jax.random.fold_in(key_list[6], 71), 0)
    query_weight = draw_query_weight(jax.random.fold_in(key_list[6], 71), 0)
    key_weight = draw_key_weight(jax.random.fold_in(key_list[6], 71), 0)
    value_weight = centred(key_list[3], (D, KV_HEADS * HEAD_DIM), D ** -0.5, 0.078125, ((1, 4),))
    output_grad = centred(key_list[4], (TOKENS, HEADS * HEAD_DIM), 8.0, 48.0, ((0, 8), (1, 4)))
    segments = jnp.searchsorted(jnp.cumsum(ragged_sizes(key_list[5], TOKENS // (2 * TOK_DEV), TOKENS, 4 * TOK_DEV, 2)), jnp.arange(TOKENS), side="right").astype(jnp.int32)
    return {"tokens": tokens, "query_weight": query_weight, "key_weight": key_weight, "value_weight": value_weight, "output_grad": output_grad, "segments": segments}


neg_large = -1e30


def block_terms(queries_blk, keys_blk, values_blk, grads_blk, query_first, key_first, seg_query, seg_key):
    tok_rows = queries_blk.shape[0]
    key_rows = keys_blk.shape[0]
    groups = HEADS // KV_HEADS
    kv_local = keys_blk.shape[1] // HEAD_DIM
    score_scale = (D / HEADS) ** -0.5
    query_four = queries_blk.reshape(tok_rows, kv_local, groups, HEAD_DIM).astype(jnp.float32)
    grad_four = grads_blk.reshape(tok_rows, kv_local, groups, HEAD_DIM).astype(jnp.float32)
    key_three = keys_blk.reshape(key_rows, kv_local, HEAD_DIM).astype(jnp.float32)
    value_three = values_blk.reshape(key_rows, kv_local, HEAD_DIM).astype(jnp.float32)
    query_pos = query_first + jnp.arange(tok_rows, dtype=jnp.int32)
    key_pos = key_first + jnp.arange(key_rows, dtype=jnp.int32)
    spacing = query_pos[:, None] - key_pos[None, :]
    allowed = (key_pos >= 0)[None, :] & (spacing >= 0) & (spacing < WINDOW) & (seg_query[:, None] == seg_key[None, :])
    scores = jnp.einsum('akgd,ckd->kgac', query_four, key_three) * score_scale
    masked = jnp.where(allowed, scores, neg_large)
    row_max = jnp.max(masked, axis=-1, keepdims=True)
    expo = jnp.where(allowed, jnp.exp(masked - row_max), 0.0)
    probs = expo / jnp.sum(expo, axis=-1, keepdims=True)
    dprobs = jnp.einsum('akgd,ckd->kgac', grad_four, value_three)
    center = jnp.sum(probs * dprobs, axis=-1, keepdims=True)
    dscores = lax.optimization_barrier((probs * (dprobs - center)).astype(jnp.bfloat16)).astype(jnp.float32)
    probs_low = lax.optimization_barrier(probs.astype(jnp.bfloat16)).astype(jnp.float32)
    query_grad = (jnp.einsum('kgac,ckd->akgd', dscores, key_three) * score_scale).reshape(tok_rows, -1).astype(jnp.bfloat16)
    key_grad = (jnp.einsum('kgac,akgd->ckd', dscores, query_four) * score_scale).reshape(key_rows, -1)
    value_grad = jnp.einsum('kgac,akgd->ckd', probs_low, grad_four).reshape(key_rows, -1)
    return query_grad, key_grad, value_grad


def reference(tokens, query_weight, key_weight, value_weight, output_grad, segments):
    queries = jnp.dot(tokens, query_weight, preferred_element_type=jnp.float32).astype(jnp.bfloat16)
    keys = jnp.dot(tokens, key_weight, preferred_element_type=jnp.float32).astype(jnp.bfloat16)
    values = jnp.dot(tokens, value_weight, preferred_element_type=jnp.float32).astype(jnp.bfloat16)
    margin = HOPS * TOK_DEV
    key_rows = (HOPS + 1) * TOK_DEV
    kv_width = key_weight.shape[1]
    pad_keys = jnp.concatenate([jnp.zeros((margin, kv_width), jnp.bfloat16), keys], axis=0)
    pad_values = jnp.concatenate([jnp.zeros((margin, kv_width), jnp.bfloat16), values], axis=0)
    pad_segs = jnp.concatenate([jnp.full((margin,), -1, jnp.int32), segments.astype(jnp.int32)], axis=0)

    def step(carried, block):
        key_acc, value_acc = carried
        offset = (block * TOK_DEV).astype(jnp.int32)
        q_blk = lax.dynamic_slice_in_dim(queries, offset, TOK_DEV, 0)
        g_blk = lax.dynamic_slice_in_dim(output_grad, offset, TOK_DEV, 0)
        k_blk = lax.dynamic_slice_in_dim(pad_keys, offset, key_rows, 0)
        v_blk = lax.dynamic_slice_in_dim(pad_values, offset, key_rows, 0)
        seg_key = lax.dynamic_slice_in_dim(pad_segs, offset, key_rows, 0)
        seg_query = lax.dynamic_slice_in_dim(segments.astype(jnp.int32), offset, TOK_DEV, 0)
        q_grad, k_grad, v_grad = block_terms(q_blk, k_blk, v_blk, g_blk, offset, offset - margin, seg_query, seg_key)
        key_acc = lax.dynamic_update_slice_in_dim(key_acc, lax.dynamic_slice_in_dim(key_acc, offset, key_rows, 0) + k_grad, offset, 0)
        value_acc = lax.dynamic_update_slice_in_dim(value_acc, lax.dynamic_slice_in_dim(value_acc, offset, key_rows, 0) + v_grad, offset, 0)
        return (key_acc, value_acc), q_grad

    start_acc = jnp.zeros((TOKENS + margin, kv_width), jnp.float32)
    (key_acc, value_acc), q_grads = lax.scan(step, (start_acc, start_acc), jnp.arange(TOKENS // TOK_DEV, dtype=jnp.int32))
    query_grad = q_grads.reshape(TOKENS, -1)
    key_grad = key_acc[margin:].astype(jnp.bfloat16)
    value_grad = value_acc[margin:].astype(jnp.bfloat16)
    q_cols = query_weight.shape[1] // N_HEAD
    k_cols = kv_width // N_HEAD
    token_sum = jnp.zeros((TOKENS, D), jnp.float32)
    for group in range(N_HEAD):
        qs = slice(group * q_cols, (group + 1) * q_cols)
        ks = slice(group * k_cols, (group + 1) * k_cols)
        partial_term = jnp.dot(query_grad[:, qs], query_weight[:, qs].T, preferred_element_type=jnp.float32)
        partial_term = partial_term + jnp.dot(key_grad[:, ks], key_weight[:, ks].T, preferred_element_type=jnp.float32)
        partial_term = partial_term + jnp.dot(value_grad[:, ks], value_weight[:, ks].T, preferred_element_type=jnp.float32)
        token_sum = token_sum + lax.optimization_barrier(partial_term.astype(jnp.bfloat16)).astype(jnp.float32)
    token_grad = token_sum.astype(jnp.bfloat16)
    grad_scale = TOKENS ** -0.5
    query_weight_grad = (jnp.dot(tokens.T, query_grad, preferred_element_type=jnp.float32) * grad_scale).astype(jnp.bfloat16)
    key_weight_grad = (jnp.dot(tokens.T, key_grad, preferred_element_type=jnp.float32) * grad_scale).astype(jnp.bfloat16)
    value_weight_grad = (jnp.dot(tokens.T, value_grad, preferred_element_type=jnp.float32) * grad_scale).astype(jnp.bfloat16)
    return (token_grad, query_weight_grad, key_weight_grad, value_weight_grad)
```

```python
import jax
import jax.numpy as jnp
from jax import lax
from jax.sharding import PartitionSpec as P

D = 5376
HEADS = 32
KV_HEADS = 16
HEAD_DIM = 128
WINDOW = 1024
HOPS = 2


neg_large = -1e30


def passed_along(x, axis, by):
    count = lax.axis_size(axis)
    pairs = [(i, i + by) for i in range(count) if 0 <= i + by < count]
    return lax.ppermute(x, axis, pairs)


def contract_last(left, right):
    return lax.dot_general(
        left, right, (((1,), (1,)), ((), ())), preferred_element_type=jnp.float32
    )


def contract_first(left, right):
    return lax.dot_general(
        left, right, (((0,), (0,)), ((), ())), preferred_element_type=jnp.float32
    )


def attend(queries, key_value, grads, query_first, key_first, seg_query, seg_key):
    tok_rows = queries.shape[0]
    key_rows = key_value.shape[1]
    groups = HEADS // KV_HEADS
    kv_local = key_value.shape[2] // HEAD_DIM
    score_scale = (D / HEADS) ** (-0.5)
    query_four = queries.reshape(tok_rows, kv_local, groups, HEAD_DIM)
    grad_four = grads.reshape(tok_rows, kv_local, groups, HEAD_DIM)
    key_three = key_value[0].reshape(key_rows, kv_local, HEAD_DIM)
    value_three = key_value[1].reshape(key_rows, kv_local, HEAD_DIM)
    query_pos = query_first + jnp.arange(tok_rows, dtype=jnp.int32)
    key_pos = key_first + jnp.arange(key_rows, dtype=jnp.int32)
    spacing = query_pos[:, None] - key_pos[None, :]
    allowed = (
        (key_pos >= 0)[None, :]
        & (spacing >= 0)
        & (spacing < WINDOW)
        & (seg_query[:, None] == seg_key[None, :])
    )
    scores = (
        jnp.einsum("akgd,ckd->kgac", query_four, key_three, preferred_element_type=jnp.float32)
        * score_scale
    )
    masked = jnp.where(allowed, scores, neg_large)
    row_max = jnp.max(masked, axis=-1, keepdims=True)
    expo = jnp.where(allowed, jnp.exp(masked - row_max), 0.0)
    probs = expo / jnp.sum(expo, axis=-1, keepdims=True)
    dprobs = jnp.einsum(
        "akgd,ckd->kgac", grad_four, value_three, preferred_element_type=jnp.float32
    )
    center = jnp.sum(probs * dprobs, axis=-1, keepdims=True)
    dscores = (probs * (dprobs - center)).astype(jnp.bfloat16)
    probs_low = probs.astype(jnp.bfloat16)
    query_grad = (
        (
            jnp.einsum("kgac,ckd->akgd", dscores, key_three, preferred_element_type=jnp.float32)
            * score_scale
        )
        .reshape(tok_rows, -1)
        .astype(jnp.bfloat16)
    )
    key_grad = (
        jnp.einsum("kgac,akgd->ckd", dscores, query_four, preferred_element_type=jnp.float32)
        * score_scale
    ).reshape(key_rows, -1)
    value_grad = jnp.einsum(
        "kgac,akgd->ckd", probs_low, grad_four, preferred_element_type=jnp.float32
    ).reshape(key_rows, -1)
    return (query_grad, jnp.stack([key_grad, value_grad]))


def per_device(tokens, query_weight, key_weight, value_weight, output_grad, segments):
    tok_rows = tokens.shape[0]
    hop_count = HOPS
    margin = hop_count * tok_rows
    gathered = lax.all_gather(tokens, "head", axis=1, tiled=True)
    queries = jnp.dot(gathered, query_weight, preferred_element_type=jnp.float32).astype(
        jnp.bfloat16
    )
    keys_own = jnp.dot(gathered, key_weight, preferred_element_type=jnp.float32).astype(
        jnp.bfloat16
    )
    values_own = jnp.dot(gathered, value_weight, preferred_element_type=jnp.float32).astype(
        jnp.bfloat16
    )
    key_value = jnp.stack([keys_own, values_own])
    blocks = [key_value] * (hop_count + 1)
    moving = key_value
    for distance in range(1, hop_count + 1):
        moving = passed_along(moving, "seq", 1)
        blocks[hop_count - distance] = moving
    keys_all = jnp.concatenate(blocks, axis=1)
    position = lax.axis_index("seq")
    query_first = position * tok_rows
    seg_query = lax.dynamic_slice_in_dim(segments, query_first, tok_rows, 0)
    seg_padded = jnp.concatenate([jnp.full((margin,), -1, jnp.int32), segments], axis=0)
    seg_key = lax.dynamic_slice_in_dim(seg_padded, query_first, (hop_count + 1) * tok_rows, 0)
    query_grad, kv_grad = attend(
        queries, keys_all, output_grad, query_first, query_first - margin, seg_query, seg_key
    )
    pieces = [
        kv_grad[:, block * tok_rows : (block + 1) * tok_rows] for block in range(hop_count + 1)
    ]
    carried = pieces[0]
    for distance in range(1, hop_count + 1):
        carried = pieces[distance] + passed_along(carried.astype(jnp.bfloat16), "seq", -1).astype(
            carried.dtype
        )
    key_grad = carried[0].astype(jnp.bfloat16)
    value_grad = carried[1].astype(jnp.bfloat16)
    n_head = lax.axis_size("head")
    me = lax.axis_index("head")
    width = tokens.shape[1]

    def term(dest):
        start = dest * width
        part = contract_last(query_grad, lax.dynamic_slice_in_dim(query_weight, start, width, 0))
        part = part + contract_last(key_grad, lax.dynamic_slice_in_dim(key_weight, start, width, 0))
        part = part + contract_last(value_grad, lax.dynamic_slice_in_dim(value_weight, start, width, 0))
        return part.astype(jnp.bfloat16)

    token_sum = None
    for shift in range(n_head - 1, 0, -1):
        sent = term((me + shift) % n_head)
        pairs = [(i, (i + shift) % n_head) for i in range(n_head)]
        got = lax.ppermute(sent, "head", pairs).astype(jnp.float32)
        token_sum = got if token_sum is None else token_sum + got
    own = term(me).astype(jnp.float32)
    token_grad = (own if token_sum is None else token_sum + own).astype(jnp.bfloat16)
    proj_grads = jnp.concatenate([query_grad, key_grad, value_grad], axis=1)
    summed = lax.psum_scatter(
        contract_first(proj_grads, gathered).astype(jnp.bfloat16),
        "seq",
        scatter_dimension=1,
        tiled=True,
    ).astype(jnp.float32)
    summed = (summed * (tok_rows * lax.axis_size("seq")) ** (-0.5)).astype(jnp.bfloat16).T
    q_width = query_weight.shape[1]
    k_width = key_weight.shape[1]
    query_weight_grad = summed[:, :q_width]
    key_weight_grad = summed[:, q_width : q_width + k_width]
    value_weight_grad = summed[:, q_width + k_width :]
    return (token_grad, query_weight_grad, key_weight_grad, value_weight_grad)


def solution(mesh):
    in_specs = (
        P("seq", "head"),
        P(None, "head"),
        P(None, "head"),
        P(None, "head"),
        P("seq", "head"),
        P(),
    )
    out_specs = (P("seq", "head"), P("seq", "head"), P("seq", "head"), P("seq", "head"))
    return jax.shard_map(
        per_device, mesh=mesh, in_specs=in_specs, out_specs=out_specs, check_vma=False
    )
```

```python
import jax
import jax.numpy as jnp
from jax import lax
from jax.sharding import Mesh, PartitionSpec as P

D = 5376
HEADS = 32
KV_HEADS = 16
HEAD_DIM = 128
WINDOW = 1024
HOPS = 2
SEQ = ("seq_hi", "core")


neg_large = -1e30


def passed_along(x, axis, by):
    count = lax.axis_size(axis)
    pairs = [(i, i + by) for i in range(count) if 0 <= i + by < count]
    return lax.ppermute(x, axis, pairs)


def contract_last(left, right):
    return lax.dot_general(
        left, right, (((1,), (1,)), ((), ())), preferred_element_type=jnp.float32
    )


def contract_first(left, right):
    return lax.dot_general(
        left, right, (((0,), (0,)), ((), ())), preferred_element_type=jnp.float32
    )


def attend(queries, key_value, grads, query_first, key_first, seg_query, seg_key):
    tok_rows = queries.shape[0]
    key_rows = key_value.shape[1]
    groups = HEADS // KV_HEADS
    kv_local = key_value.shape[2] // HEAD_DIM
    score_scale = (D / HEADS) ** (-0.5)
    query_four = queries.reshape(tok_rows, kv_local, groups, HEAD_DIM)
    grad_four = grads.reshape(tok_rows, kv_local, groups, HEAD_DIM)
    key_three = key_value[0].reshape(key_rows, kv_local, HEAD_DIM)
    value_three = key_value[1].reshape(key_rows, kv_local, HEAD_DIM)
    query_pos = query_first + jnp.arange(tok_rows, dtype=jnp.int32)
    key_pos = key_first + jnp.arange(key_rows, dtype=jnp.int32)
    spacing = query_pos[:, None] - key_pos[None, :]
    allowed = (
        (key_pos >= 0)[None, :]
        & (spacing >= 0)
        & (spacing < WINDOW)
        & (seg_query[:, None] == seg_key[None, :])
    )
    scores = (
        jnp.einsum("akgd,ckd->kgac", query_four, key_three, preferred_element_type=jnp.float32)
        * score_scale
    )
    masked = jnp.where(allowed, scores, neg_large)
    row_max = jnp.max(masked, axis=-1, keepdims=True)
    expo = jnp.where(allowed, jnp.exp(masked - row_max), 0.0)
    probs = expo / jnp.sum(expo, axis=-1, keepdims=True)
    dprobs = jnp.einsum(
        "akgd,ckd->kgac", grad_four, value_three, preferred_element_type=jnp.float32
    )
    center = jnp.sum(probs * dprobs, axis=-1, keepdims=True)
    dscores = (probs * (dprobs - center)).astype(jnp.bfloat16)
    probs_low = probs.astype(jnp.bfloat16)
    query_grad = (
        (
            jnp.einsum("kgac,ckd->akgd", dscores, key_three, preferred_element_type=jnp.float32)
            * score_scale
        )
        .reshape(tok_rows, -1)
        .astype(jnp.bfloat16)
    )
    key_grad = (
        jnp.einsum("kgac,akgd->ckd", dscores, query_four, preferred_element_type=jnp.float32)
        * score_scale
    ).reshape(key_rows, -1)
    value_grad = jnp.einsum(
        "kgac,akgd->ckd", probs_low, grad_four, preferred_element_type=jnp.float32
    ).reshape(key_rows, -1)
    return (query_grad, jnp.stack([key_grad, value_grad]))


def per_device(tokens, query_weight, key_weight, value_weight, output_grad, segments):
    tok_rows = tokens.shape[0]
    hop_count = HOPS
    margin = hop_count * tok_rows
    gathered = lax.all_gather(tokens, "head", axis=1, tiled=True)
    queries = jnp.dot(gathered, query_weight, preferred_element_type=jnp.float32).astype(
        jnp.bfloat16
    )
    keys_own = jnp.dot(gathered, key_weight, preferred_element_type=jnp.float32).astype(
        jnp.bfloat16
    )
    values_own = jnp.dot(gathered, value_weight, preferred_element_type=jnp.float32).astype(
        jnp.bfloat16
    )
    key_value = jnp.stack([keys_own, values_own])
    blocks = [key_value] * (hop_count + 1)
    for distance in range(1, hop_count + 1):
        blocks[hop_count - distance] = passed_along(key_value, SEQ, distance)
    keys_all = jnp.concatenate(blocks, axis=1)
    position = lax.axis_index(SEQ)
    query_first = position * tok_rows
    seg_query = lax.dynamic_slice_in_dim(segments, query_first, tok_rows, 0)
    seg_padded = jnp.concatenate([jnp.full((margin,), -1, jnp.int32), segments], axis=0)
    seg_key = lax.dynamic_slice_in_dim(seg_padded, query_first, (hop_count + 1) * tok_rows, 0)
    query_grad, kv_grad = attend(
        queries, keys_all, output_grad, query_first, query_first - margin, seg_query, seg_key
    )
    pieces = [
        kv_grad[:, block * tok_rows : (block + 1) * tok_rows] for block in range(hop_count + 1)
    ]
    carried = pieces[hop_count]
    for distance in range(1, hop_count + 1):
        back = passed_along(pieces[hop_count - distance].astype(jnp.bfloat16), SEQ, -distance)
        carried = carried + back.astype(jnp.float32)
    key_grad = carried[0].astype(jnp.bfloat16)
    value_grad = carried[1].astype(jnp.bfloat16)
    n_head = lax.axis_size("head")
    me = lax.axis_index("head")
    width = tokens.shape[1]

    def term(dest):
        start = dest * width
        part = contract_last(query_grad, lax.dynamic_slice_in_dim(query_weight, start, width, 0))
        part = part + contract_last(key_grad, lax.dynamic_slice_in_dim(key_weight, start, width, 0))
        part = part + contract_last(value_grad, lax.dynamic_slice_in_dim(value_weight, start, width, 0))
        return part.astype(jnp.bfloat16)

    token_sum = None
    for shift in range(n_head - 1, 0, -1):
        sent = term((me + shift) % n_head)
        pairs = [(i, (i + shift) % n_head) for i in range(n_head)]
        got = lax.ppermute(sent, "head", pairs).astype(jnp.float32)
        token_sum = got if token_sum is None else token_sum + got
    own = term(me).astype(jnp.float32)
    token_grad = (own if token_sum is None else token_sum + own).astype(jnp.bfloat16)
    proj_grads = jnp.concatenate([query_grad, key_grad, value_grad], axis=1)
    weight_part = contract_first(proj_grads, gathered)
    n_hi = lax.axis_size("seq_hi")
    quarter = weight_part.reshape(weight_part.shape[0], n_hi, 2, -1)
    core = lax.axis_index("core")
    keep = lax.dynamic_index_in_dim(quarter, core, 2, keepdims=False)
    give = lax.dynamic_index_in_dim(quarter, 1 - core, 2, keepdims=False).astype(jnp.bfloat16)
    got = lax.ppermute(give, "core", [(0, 1), (1, 0)])
    pair_sum = (keep + got.astype(jnp.float32)).astype(jnp.bfloat16)
    summed = lax.psum_scatter(pair_sum, "seq_hi", scatter_dimension=1, tiled=True)
    summed = summed.reshape(summed.shape[0], -1).astype(jnp.float32)
    summed = (summed * (tok_rows * lax.axis_size(SEQ)) ** (-0.5)).astype(jnp.bfloat16).T
    q_width = query_weight.shape[1]
    k_width = key_weight.shape[1]
    query_weight_grad = summed[:, :q_width]
    key_weight_grad = summed[:, q_width : q_width + k_width]
    value_weight_grad = summed[:, q_width + k_width :]
    return (token_grad, query_weight_grad, key_weight_grad, value_weight_grad)


def solution(mesh):
    n_seq = mesh.shape["seq"]
    n_head = mesh.shape["head"]
    view = Mesh(mesh.devices.reshape(n_seq // 2, 2, n_head), ("seq_hi", "core", "head"))
    in_specs = (
        P(SEQ, "head"),
        P(None, "head"),
        P(None, "head"),
        P(None, "head"),
        P(SEQ, "head"),
        P(),
    )
    out_specs = (P(SEQ, "head"),) * 4
    return jax.shard_map(
        per_device, mesh=view, in_specs=in_specs, out_specs=out_specs, check_vma=False
    )
```

```python
import jax
import jax.numpy as jnp
from jax import lax
from jax.sharding import Mesh, PartitionSpec as P

D = 5376
HEADS = 32
KV_HEADS = 16
HEAD_DIM = 128
WINDOW = 1024
HOPS = 2
SEQ = ("seq_hi", "core")


neg_large = -1e30


def passed_along(x, axis, by):
    count = lax.axis_size(axis)
    pairs = [(i, i + by) for i in range(count) if 0 <= i + by < count]
    return lax.ppermute(x, axis, pairs)


def contract_last(left, right):
    return lax.dot_general(
        left, right, (((1,), (1,)), ((), ())), preferred_element_type=jnp.float32
    )


def contract_first(left, right):
    return lax.dot_general(
        left, right, (((0,), (0,)), ((), ())), preferred_element_type=jnp.float32
    )


def attend(queries, key_value, grads, query_first, key_first, seg_query, seg_key):
    tok_rows = queries.shape[0]
    key_rows = key_value.shape[1]
    groups = HEADS // KV_HEADS
    kv_local = key_value.shape[2] // HEAD_DIM
    score_scale = (D / HEADS) ** (-0.5)
    query_four = queries.reshape(tok_rows, kv_local, groups, HEAD_DIM)
    grad_four = grads.reshape(tok_rows, kv_local, groups, HEAD_DIM)
    key_three = key_value[0].reshape(key_rows, kv_local, HEAD_DIM)
    value_three = key_value[1].reshape(key_rows, kv_local, HEAD_DIM)
    query_pos = query_first + jnp.arange(tok_rows, dtype=jnp.int32)
    key_pos = key_first + jnp.arange(key_rows, dtype=jnp.int32)
    spacing = query_pos[:, None] - key_pos[None, :]
    allowed = (
        (key_pos >= 0)[None, :]
        & (spacing >= 0)
        & (spacing < WINDOW)
        & (seg_query[:, None] == seg_key[None, :])
    )
    scores = (
        jnp.einsum("akgd,ckd->kgac", query_four, key_three, preferred_element_type=jnp.float32)
        * score_scale
    )
    masked = jnp.where(allowed, scores, neg_large)
    row_max = jnp.max(masked, axis=-1, keepdims=True)
    expo = jnp.where(allowed, jnp.exp(masked - row_max), 0.0)
    probs = expo / jnp.sum(expo, axis=-1, keepdims=True)
    dprobs = jnp.einsum(
        "akgd,ckd->kgac", grad_four, value_three, preferred_element_type=jnp.float32
    )
    center = jnp.sum(probs * dprobs, axis=-1, keepdims=True)
    dscores = (probs * (dprobs - center)).astype(jnp.bfloat16)
    probs_low = probs.astype(jnp.bfloat16)
    query_grad = (
        (
            jnp.einsum("kgac,ckd->akgd", dscores, key_three, preferred_element_type=jnp.float32)
            * score_scale
        )
        .reshape(tok_rows, -1)
        .astype(jnp.bfloat16)
    )
    key_grad = (
        jnp.einsum("kgac,akgd->ckd", dscores, query_four, preferred_element_type=jnp.float32)
        * score_scale
    ).reshape(key_rows, -1)
    value_grad = jnp.einsum(
        "kgac,akgd->ckd", probs_low, grad_four, preferred_element_type=jnp.float32
    ).reshape(key_rows, -1)
    return (query_grad, jnp.stack([key_grad, value_grad]))


def per_device(tokens, query_weight, key_weight, value_weight, output_grad, segments):
    tok_rows = tokens.shape[0]
    hop_count = HOPS
    margin = hop_count * tok_rows
    gathered = lax.all_gather(tokens, "head", axis=1, tiled=True)
    queries = jnp.dot(gathered, query_weight, preferred_element_type=jnp.float32).astype(
        jnp.bfloat16
    )
    keys_own = jnp.dot(gathered, key_weight, preferred_element_type=jnp.float32).astype(
        jnp.bfloat16
    )
    values_own = jnp.dot(gathered, value_weight, preferred_element_type=jnp.float32).astype(
        jnp.bfloat16
    )
    key_value = jnp.stack([keys_own, values_own])
    blocks = [key_value] * (hop_count + 1)
    for distance in range(1, hop_count + 1):
        blocks[hop_count - distance] = passed_along(key_value, SEQ, distance)
    keys_all = jnp.concatenate(blocks, axis=1)
    position = lax.axis_index(SEQ)
    query_first = position * tok_rows
    seg_query = lax.dynamic_slice_in_dim(segments, query_first, tok_rows, 0)
    seg_padded = jnp.concatenate([jnp.full((margin,), -1, jnp.int32), segments], axis=0)
    seg_key = lax.dynamic_slice_in_dim(seg_padded, query_first, (hop_count + 1) * tok_rows, 0)
    query_grad, kv_grad = attend(
        queries, keys_all, output_grad, query_first, query_first - margin, seg_query, seg_key
    )
    pieces = [
        kv_grad[:, block * tok_rows : (block + 1) * tok_rows] for block in range(hop_count + 1)
    ]
    carried = pieces[hop_count]
    for distance in range(1, hop_count + 1):
        back = passed_along(pieces[hop_count - distance].astype(jnp.bfloat16), SEQ, -distance)
        carried = carried + back.astype(jnp.float32)
    key_grad = carried[0].astype(jnp.bfloat16)
    value_grad = carried[1].astype(jnp.bfloat16)
    n_head = lax.axis_size("head")
    me = lax.axis_index("head")
    width = tokens.shape[1]

    def term(dest):
        start = dest * width
        part = contract_last(query_grad, lax.dynamic_slice_in_dim(query_weight, start, width, 0))
        part = part + contract_last(key_grad, lax.dynamic_slice_in_dim(key_weight, start, width, 0))
        part = part + contract_last(value_grad, lax.dynamic_slice_in_dim(value_weight, start, width, 0))
        return part.astype(jnp.bfloat16)

    token_sum = None
    for shift in range(n_head - 1, 0, -1):
        sent = term((me + shift) % n_head)
        pairs = [(i, (i + shift) % n_head) for i in range(n_head)]
        got = lax.ppermute(sent, "head", pairs).astype(jnp.float32)
        token_sum = got if token_sum is None else token_sum + got
    own = term(me).astype(jnp.float32)
    token_grad = (own if token_sum is None else token_sum + own).astype(jnp.bfloat16)
    proj_grads = jnp.concatenate([query_grad, key_grad, value_grad], axis=1)
    n_hi = lax.axis_size("seq_hi")
    core = lax.axis_index("core")
    swap = [(0, 1), (1, 0)]
    halves = gathered.reshape(tok_rows, n_hi, 2, -1)
    own_cols = lax.dynamic_index_in_dim(halves, core, 2, keepdims=False).reshape(tok_rows, -1)
    partner_cols = lax.dynamic_index_in_dim(halves, 1 - core, 2, keepdims=False).reshape(tok_rows, -1)
    partner_tokens = lax.ppermute(partner_cols, "core", swap)
    partner_grads = lax.ppermute(proj_grads, "core", swap)
    pair_tokens = jnp.concatenate([own_cols, partner_tokens], axis=0)
    pair_grads = jnp.concatenate([proj_grads, partner_grads], axis=0)
    pair_sum = contract_first(pair_grads, pair_tokens).astype(jnp.bfloat16)
    pair_sum = pair_sum.reshape(pair_sum.shape[0], n_hi, -1)
    summed = lax.psum_scatter(pair_sum, "seq_hi", scatter_dimension=1, tiled=True)
    summed = summed.reshape(summed.shape[0], -1).astype(jnp.float32)
    summed = (summed * (tok_rows * lax.axis_size(SEQ)) ** (-0.5)).astype(jnp.bfloat16).T
    q_width = query_weight.shape[1]
    k_width = key_weight.shape[1]
    query_weight_grad = summed[:, :q_width]
    key_weight_grad = summed[:, q_width : q_width + k_width]
    value_weight_grad = summed[:, q_width + k_width :]
    return (token_grad, query_weight_grad, key_weight_grad, value_weight_grad)


def solution(mesh):
    n_seq = mesh.shape["seq"]
    n_head = mesh.shape["head"]
    view = Mesh(mesh.devices.reshape(n_seq // 2, 2, n_head), ("seq_hi", "core", "head"))
    in_specs = (
        P(SEQ, "head"),
        P(None, "head"),
        P(None, "head"),
        P(None, "head"),
        P(SEQ, "head"),
        P(),
    )
    out_specs = (P(SEQ, "head"),) * 4
    return jax.shard_map(
        per_device, mesh=view, in_specs=in_specs, out_specs=out_specs, check_vma=False
    )
```

```python
import jax
import jax.numpy as jnp
from jax import lax
from jax.sharding import Mesh, PartitionSpec as P

D = 5376
HEADS = 32
KV_HEADS = 16
HEAD_DIM = 128
WINDOW = 1024
HOPS = 2
SEQ = ("seq_hi", "core")


neg_large = -1e30


def passed_along(x, axis, by):
    count = lax.axis_size(axis)
    pairs = [(i, i + by) for i in range(count) if 0 <= i + by < count]
    return lax.ppermute(x, axis, pairs)


def contract_last(left, right):
    return lax.dot_general(
        left, right, (((1,), (1,)), ((), ())), preferred_element_type=jnp.float32
    )


def contract_first(left, right):
    return lax.dot_general(
        left, right, (((0,), (0,)), ((), ())), preferred_element_type=jnp.float32
    )


def attend(queries, key_value, grads, query_first, key_first, seg_query, seg_key):
    tok_rows = queries.shape[0]
    key_rows = key_value.shape[1]
    groups = HEADS // KV_HEADS
    kv_local = key_value.shape[2] // HEAD_DIM
    score_scale = (D / HEADS) ** (-0.5)
    query_four = queries.reshape(tok_rows, kv_local, groups, HEAD_DIM)
    grad_four = grads.reshape(tok_rows, kv_local, groups, HEAD_DIM)
    key_three = key_value[0].reshape(key_rows, kv_local, HEAD_DIM)
    value_three = key_value[1].reshape(key_rows, kv_local, HEAD_DIM)
    query_pos = query_first + jnp.arange(tok_rows, dtype=jnp.int32)
    key_pos = key_first + jnp.arange(key_rows, dtype=jnp.int32)
    spacing = query_pos[:, None] - key_pos[None, :]
    allowed = (
        (key_pos >= 0)[None, :]
        & (spacing >= 0)
        & (spacing < WINDOW)
        & (seg_query[:, None] == seg_key[None, :])
    )
    scores = (
        jnp.einsum("akgd,ckd->kgac", query_four, key_three, preferred_element_type=jnp.float32)
        * score_scale
    )
    masked = jnp.where(allowed, scores, neg_large)
    row_max = jnp.max(masked, axis=-1, keepdims=True)
    expo = jnp.where(allowed, jnp.exp(masked - row_max), 0.0)
    probs = expo / jnp.sum(expo, axis=-1, keepdims=True)
    dprobs = jnp.einsum(
        "akgd,ckd->kgac", grad_four, value_three, preferred_element_type=jnp.float32
    )
    center = jnp.sum(probs * dprobs, axis=-1, keepdims=True)
    dscores = (probs * (dprobs - center)).astype(jnp.bfloat16)
    probs_low = probs.astype(jnp.bfloat16)
    query_grad = (
        (
            jnp.einsum("kgac,ckd->akgd", dscores, key_three, preferred_element_type=jnp.float32)
            * score_scale
        )
        .reshape(tok_rows, -1)
        .astype(jnp.bfloat16)
    )
    key_grad = (
        jnp.einsum("kgac,akgd->ckd", dscores, query_four, preferred_element_type=jnp.float32)
        * score_scale
    ).reshape(key_rows, -1)
    value_grad = jnp.einsum(
        "kgac,akgd->ckd", probs_low, grad_four, preferred_element_type=jnp.float32
    ).reshape(key_rows, -1)
    return (query_grad, jnp.stack([key_grad, value_grad]))


def per_device(tokens, query_weight, key_weight, value_weight, output_grad, segments):
    tok_rows = tokens.shape[0]
    hop_count = HOPS
    margin = hop_count * tok_rows
    gathered = lax.all_gather(tokens, "head", axis=1, tiled=True)
    queries = jnp.dot(gathered, query_weight, preferred_element_type=jnp.float32).astype(
        jnp.bfloat16
    )
    keys_own = jnp.dot(gathered, key_weight, preferred_element_type=jnp.float32).astype(
        jnp.bfloat16
    )
    values_own = jnp.dot(gathered, value_weight, preferred_element_type=jnp.float32).astype(
        jnp.bfloat16
    )
    key_value = jnp.stack([keys_own, values_own])
    blocks = [key_value] * (hop_count + 1)
    for distance in range(1, hop_count + 1):
        blocks[hop_count - distance] = passed_along(key_value, SEQ, distance)
    keys_all = jnp.concatenate(blocks, axis=1)
    position = lax.axis_index(SEQ)
    query_first = position * tok_rows
    seg_query = lax.dynamic_slice_in_dim(segments, query_first, tok_rows, 0)
    seg_padded = jnp.concatenate([jnp.full((margin,), -1, jnp.int32), segments], axis=0)
    seg_key = lax.dynamic_slice_in_dim(seg_padded, query_first, (hop_count + 1) * tok_rows, 0)
    query_grad, kv_grad = attend(
        queries, keys_all, output_grad, query_first, query_first - margin, seg_query, seg_key
    )
    pieces = [
        kv_grad[:, block * tok_rows : (block + 1) * tok_rows] for block in range(hop_count + 1)
    ]
    carried = pieces[hop_count]
    for distance in range(1, hop_count + 1):
        back = passed_along(pieces[hop_count - distance].astype(jnp.bfloat16), SEQ, -distance)
        carried = carried + back.astype(jnp.float32)
    key_grad = carried[0].astype(jnp.bfloat16)
    value_grad = carried[1].astype(jnp.bfloat16)
    n_head = lax.axis_size("head")
    me = lax.axis_index("head")
    width = tokens.shape[1]

    def term(dest):
        start = dest * width
        part = contract_last(query_grad, lax.dynamic_slice_in_dim(query_weight, start, width, 0))
        part = part + contract_last(key_grad, lax.dynamic_slice_in_dim(key_weight, start, width, 0))
        part = part + contract_last(value_grad, lax.dynamic_slice_in_dim(value_weight, start, width, 0))
        return part.astype(jnp.bfloat16)

    token_sum = None
    for shift in range(n_head - 1, 0, -1):
        sent = term((me + shift) % n_head)
        pairs = [(i, (i + shift) % n_head) for i in range(n_head)]
        got = lax.ppermute(sent, "head", pairs).astype(jnp.float32)
        token_sum = got if token_sum is None else token_sum + got
    own = term(me).astype(jnp.float32)
    token_grad = (own if token_sum is None else token_sum + own).astype(jnp.bfloat16)
    n_hi = lax.axis_size("seq_hi")
    core = lax.axis_index("core")
    swap = [(0, 1), (1, 0)]
    halves = gathered.reshape(tok_rows, n_hi, 2, -1)
    own_cols = lax.dynamic_index_in_dim(halves, core, 2, keepdims=False).reshape(tok_rows, -1)
    partner_cols = lax.dynamic_index_in_dim(halves, 1 - core, 2, keepdims=False).reshape(tok_rows, -1)
    pair_tokens = jnp.concatenate([own_cols, lax.ppermute(partner_cols, "core", swap)], axis=0)
    weight_scale = (tok_rows * lax.axis_size(SEQ)) ** (-0.5)

    def weight_grad(grads):
        pair_grads = jnp.concatenate([grads, lax.ppermute(grads, "core", swap)], axis=0)
        pair_sum = contract_first(pair_grads, pair_tokens).astype(jnp.bfloat16)
        summed = lax.psum_scatter(pair_sum, "seq_hi", scatter_dimension=1, tiled=True)
        return (summed.astype(jnp.float32) * weight_scale).astype(jnp.bfloat16).T

    query_weight_grad = weight_grad(query_grad)
    kv_weight_grad = weight_grad(jnp.concatenate([key_grad, value_grad], axis=1))
    k_width = key_weight.shape[1]
    key_weight_grad = kv_weight_grad[:, :k_width]
    value_weight_grad = kv_weight_grad[:, k_width:]
    return (token_grad, query_weight_grad, key_weight_grad, value_weight_grad)


def solution(mesh):
    n_seq = mesh.shape["seq"]
    n_head = mesh.shape["head"]
    view = Mesh(mesh.devices.reshape(n_seq // 2, 2, n_head), ("seq_hi", "core", "head"))
    in_specs = (
        P(SEQ, "head"),
        P(None, "head"),
        P(None, "head"),
        P(None, "head"),
        P(SEQ, "head"),
        P(),
    )
    out_specs = (P(SEQ, "head"),) * 4
    return jax.shard_map(
        per_device, mesh=view, in_specs=in_specs, out_specs=out_specs, check_vma=False
    )
```

```python
import jax
import jax.numpy as jnp
from jax import lax
from jax.sharding import Mesh, PartitionSpec as P

D = 5376
HEADS = 32
KV_HEADS = 16
HEAD_DIM = 128
WINDOW = 1024
HOPS = 2
SEQ = ("seq_hi", "core")


neg_large = -1e30


def passed_along(x, axis, by):
    count = lax.axis_size(axis)
    pairs = [(i, i + by) for i in range(count) if 0 <= i + by < count]
    return lax.ppermute(x, axis, pairs)


def contract_last(left, right):
    return lax.dot_general(
        left, right, (((1,), (1,)), ((), ())), preferred_element_type=jnp.float32
    )


def contract_first(left, right):
    return lax.dot_general(
        left, right, (((0,), (0,)), ((), ())), preferred_element_type=jnp.float32
    )


def attend(queries, key_value, grads, query_first, key_first, seg_query, seg_key):
    tok_rows = queries.shape[0]
    key_rows = key_value.shape[1]
    groups = HEADS // KV_HEADS
    kv_local = key_value.shape[2] // HEAD_DIM
    score_scale = (D / HEADS) ** (-0.5)
    query_four = queries.reshape(tok_rows, kv_local, groups, HEAD_DIM)
    grad_four = grads.reshape(tok_rows, kv_local, groups, HEAD_DIM)
    key_three = key_value[0].reshape(key_rows, kv_local, HEAD_DIM)
    value_three = key_value[1].reshape(key_rows, kv_local, HEAD_DIM)
    query_pos = query_first + jnp.arange(tok_rows, dtype=jnp.int32)
    key_pos = key_first + jnp.arange(key_rows, dtype=jnp.int32)
    spacing = query_pos[:, None] - key_pos[None, :]
    allowed = (
        (key_pos >= 0)[None, :]
        & (spacing >= 0)
        & (spacing < WINDOW)
        & (seg_query[:, None] == seg_key[None, :])
    )
    scores = (
        jnp.einsum("akgd,ckd->kgac", query_four, key_three, preferred_element_type=jnp.float32)
        * score_scale
    )
    masked = jnp.where(allowed, scores, neg_large)
    row_max = jnp.max(masked, axis=-1, keepdims=True)
    expo = jnp.where(allowed, jnp.exp(masked - row_max), 0.0)
    probs = expo / jnp.sum(expo, axis=-1, keepdims=True)
    dprobs = jnp.einsum(
        "akgd,ckd->kgac", grad_four, value_three, preferred_element_type=jnp.float32
    )
    center = jnp.sum(probs * dprobs, axis=-1, keepdims=True)
    dscores = (probs * (dprobs - center)).astype(jnp.bfloat16)
    probs_low = probs.astype(jnp.bfloat16)
    query_grad = (
        (
            jnp.einsum("kgac,ckd->akgd", dscores, key_three, preferred_element_type=jnp.float32)
            * score_scale
        )
        .reshape(tok_rows, -1)
        .astype(jnp.bfloat16)
    )
    key_grad = (
        jnp.einsum("kgac,akgd->ckd", dscores, query_four, preferred_element_type=jnp.float32)
        * score_scale
    ).reshape(key_rows, -1)
    value_grad = jnp.einsum(
        "kgac,akgd->ckd", probs_low, grad_four, preferred_element_type=jnp.float32
    ).reshape(key_rows, -1)
    return (query_grad, jnp.stack([key_grad, value_grad]))


def per_device(tokens, query_weight, key_weight, value_weight, output_grad, segments):
    tok_rows = tokens.shape[0]
    hop_count = HOPS
    margin = hop_count * tok_rows
    gathered = lax.all_gather(tokens, "head", axis=1, tiled=True)
    queries = jnp.dot(gathered, query_weight, preferred_element_type=jnp.float32).astype(
        jnp.bfloat16
    )
    keys_own = jnp.dot(gathered, key_weight, preferred_element_type=jnp.float32).astype(
        jnp.bfloat16
    )
    values_own = jnp.dot(gathered, value_weight, preferred_element_type=jnp.float32).astype(
        jnp.bfloat16
    )
    key_value = jnp.stack([keys_own, values_own])
    blocks = [key_value] * (hop_count + 1)
    for distance in range(1, hop_count + 1):
        blocks[hop_count - distance] = passed_along(key_value, SEQ, distance)
    keys_all = jnp.concatenate(blocks, axis=1)
    position = lax.axis_index(SEQ)
    query_first = position * tok_rows
    seg_query = lax.dynamic_slice_in_dim(segments, query_first, tok_rows, 0)
    seg_padded = jnp.concatenate([jnp.full((margin,), -1, jnp.int32), segments], axis=0)
    seg_key = lax.dynamic_slice_in_dim(seg_padded, query_first, (hop_count + 1) * tok_rows, 0)
    query_grad, kv_grad = attend(
        queries, keys_all, output_grad, query_first, query_first - margin, seg_query, seg_key
    )
    pieces = [
        kv_grad[:, block * tok_rows : (block + 1) * tok_rows] for block in range(hop_count + 1)
    ]
    carried = pieces[hop_count]
    for distance in range(1, hop_count + 1):
        back = passed_along(pieces[hop_count - distance].astype(jnp.bfloat16), SEQ, -distance)
        carried = carried + back.astype(jnp.float32)
    key_grad = carried[0].astype(jnp.bfloat16)
    value_grad = carried[1].astype(jnp.bfloat16)
    n_head = lax.axis_size("head")
    me = lax.axis_index("head")
    width = tokens.shape[1]

    def term(dest):
        start = dest * width
        part = contract_last(query_grad, lax.dynamic_slice_in_dim(query_weight, start, width, 0))
        part = part + contract_last(key_grad, lax.dynamic_slice_in_dim(key_weight, start, width, 0))
        part = part + contract_last(value_grad, lax.dynamic_slice_in_dim(value_weight, start, width, 0))
        return part.astype(jnp.bfloat16)

    token_sum = None
    for shift in range(n_head - 1, 0, -1):
        sent = term((me + shift) % n_head)
        pairs = [(i, (i + shift) % n_head) for i in range(n_head)]
        got = lax.ppermute(sent, "head", pairs).astype(jnp.float32)
        token_sum = got if token_sum is None else token_sum + got
    own = term(me).astype(jnp.float32)
    token_grad = (own if token_sum is None else token_sum + own).astype(jnp.bfloat16)
    proj_grads = jnp.concatenate([query_grad, key_grad, value_grad], axis=1)
    weight_part = contract_first(proj_grads, gathered).astype(jnp.bfloat16)
    n_seq = lax.axis_size(SEQ)
    block = weight_part.shape[1] // n_seq

    def weight_block(dest):
        return lax.dynamic_slice_in_dim(weight_part, dest * block, block, 1)

    weight_sum = weight_block(position).astype(jnp.float32)
    for shift in range(n_seq - 1, 0, -1):
        sent = weight_block((position + shift) % n_seq)
        pairs = [(i, (i + shift) % n_seq) for i in range(n_seq)]
        weight_sum = weight_sum + lax.ppermute(sent, SEQ, pairs).astype(jnp.float32)
    summed = (weight_sum * (tok_rows * n_seq) ** (-0.5)).astype(jnp.bfloat16).T
    q_width = query_weight.shape[1]
    k_width = key_weight.shape[1]
    query_weight_grad = summed[:, :q_width]
    key_weight_grad = summed[:, q_width : q_width + k_width]
    value_weight_grad = summed[:, q_width + k_width :]
    return (token_grad, query_weight_grad, key_weight_grad, value_weight_grad)


def solution(mesh):
    n_seq = mesh.shape["seq"]
    n_head = mesh.shape["head"]
    view = Mesh(mesh.devices.reshape(n_seq // 2, 2, n_head), ("seq_hi", "core", "head"))
    in_specs = (
        P(SEQ, "head"),
        P(None, "head"),
        P(None, "head"),
        P(None, "head"),
        P(SEQ, "head"),
        P(),
    )
    out_specs = (P(SEQ, "head"),) * 4
    return jax.shard_map(
        per_device, mesh=view, in_specs=in_specs, out_specs=out_specs, check_vma=False
    )
```

```python
import jax
import jax.numpy as jnp
from jax import lax
from jax.sharding import Mesh, PartitionSpec as P

D = 5376
HEADS = 32
KV_HEADS = 16
HEAD_DIM = 128
WINDOW = 1024
HOPS = 2
SEQ = ("seq_hi", "core")


neg_large = -1e30


def passed_along(x, axis, by):
    count = lax.axis_size(axis)
    pairs = [(i, i + by) for i in range(count) if 0 <= i + by < count]
    return lax.ppermute(x, axis, pairs)


def contract_last(left, right):
    return lax.dot_general(
        left, right, (((1,), (1,)), ((), ())), preferred_element_type=jnp.float32
    )


def contract_first(left, right):
    return lax.dot_general(
        left, right, (((0,), (0,)), ((), ())), preferred_element_type=jnp.float32
    )


def attend(queries, key_value, grads, query_first, key_first, seg_query, seg_key):
    tok_rows = queries.shape[0]
    key_rows = key_value.shape[1]
    groups = HEADS // KV_HEADS
    kv_local = key_value.shape[2] // HEAD_DIM
    score_scale = (D / HEADS) ** (-0.5)
    query_four = queries.reshape(tok_rows, kv_local, groups, HEAD_DIM)
    grad_four = grads.reshape(tok_rows, kv_local, groups, HEAD_DIM)
    key_three = key_value[0].reshape(key_rows, kv_local, HEAD_DIM)
    value_three = key_value[1].reshape(key_rows, kv_local, HEAD_DIM)
    query_pos = query_first + jnp.arange(tok_rows, dtype=jnp.int32)
    key_pos = key_first + jnp.arange(key_rows, dtype=jnp.int32)
    spacing = query_pos[:, None] - key_pos[None, :]
    allowed = (
        (key_pos >= 0)[None, :]
        & (spacing >= 0)
        & (spacing < WINDOW)
        & (seg_query[:, None] == seg_key[None, :])
    )
    scores = (
        jnp.einsum("akgd,ckd->kgac", query_four, key_three, preferred_element_type=jnp.float32)
        * score_scale
    )
    masked = jnp.where(allowed, scores, neg_large)
    row_max = jnp.max(masked, axis=-1, keepdims=True)
    expo = jnp.where(allowed, jnp.exp(masked - row_max), 0.0)
    probs = expo / jnp.sum(expo, axis=-1, keepdims=True)
    dprobs = jnp.einsum(
        "akgd,ckd->kgac", grad_four, value_three, preferred_element_type=jnp.float32
    )
    center = jnp.sum(probs * dprobs, axis=-1, keepdims=True)
    dscores = (probs * (dprobs - center)).astype(jnp.bfloat16)
    probs_low = probs.astype(jnp.bfloat16)
    query_grad = (
        (
            jnp.einsum("kgac,ckd->akgd", dscores, key_three, preferred_element_type=jnp.float32)
            * score_scale
        )
        .reshape(tok_rows, -1)
        .astype(jnp.bfloat16)
    )
    key_grad = (
        jnp.einsum("kgac,akgd->ckd", dscores, query_four, preferred_element_type=jnp.float32)
        * score_scale
    ).reshape(key_rows, -1)
    value_grad = jnp.einsum(
        "kgac,akgd->ckd", probs_low, grad_four, preferred_element_type=jnp.float32
    ).reshape(key_rows, -1)
    return (query_grad, jnp.stack([key_grad, value_grad]))


def per_device(tokens, query_weight, key_weight, value_weight, output_grad, segments):
    tok_rows = tokens.shape[0]
    hop_count = HOPS
    margin = hop_count * tok_rows
    gathered = lax.all_gather(tokens, "head", axis=1, tiled=True)
    queries = jnp.dot(gathered, query_weight, preferred_element_type=jnp.float32).astype(
        jnp.bfloat16
    )
    keys_own = jnp.dot(gathered, key_weight, preferred_element_type=jnp.float32).astype(
        jnp.bfloat16
    )
    values_own = jnp.dot(gathered, value_weight, preferred_element_type=jnp.float32).astype(
        jnp.bfloat16
    )
    key_value = jnp.stack([keys_own, values_own])
    blocks = [key_value] * (hop_count + 1)
    for distance in range(1, hop_count + 1):
        blocks[hop_count - distance] = passed_along(key_value, SEQ, distance)
    keys_all = jnp.concatenate(blocks, axis=1)
    position = lax.axis_index(SEQ)
    query_first = position * tok_rows
    seg_query = lax.dynamic_slice_in_dim(segments, query_first, tok_rows, 0)
    seg_padded = jnp.concatenate([jnp.full((margin,), -1, jnp.int32), segments], axis=0)
    seg_key = lax.dynamic_slice_in_dim(seg_padded, query_first, (hop_count + 1) * tok_rows, 0)
    query_grad, kv_grad = attend(
        queries, keys_all, output_grad, query_first, query_first - margin, seg_query, seg_key
    )
    pieces = [
        kv_grad[:, block * tok_rows : (block + 1) * tok_rows] for block in range(hop_count + 1)
    ]
    carried = pieces[hop_count]
    for distance in range(1, hop_count + 1):
        back = passed_along(pieces[hop_count - distance].astype(jnp.bfloat16), SEQ, -distance)
        carried = carried + back.astype(jnp.float32)
    key_grad = carried[0].astype(jnp.bfloat16)
    value_grad = carried[1].astype(jnp.bfloat16)
    n_head = lax.axis_size("head")
    me = lax.axis_index("head")
    width = tokens.shape[1]

    def term(dest):
        start = dest * width
        part = contract_last(query_grad, lax.dynamic_slice_in_dim(query_weight, start, width, 0))
        part = part + contract_last(key_grad, lax.dynamic_slice_in_dim(key_weight, start, width, 0))
        part = part + contract_last(value_grad, lax.dynamic_slice_in_dim(value_weight, start, width, 0))
        return part.astype(jnp.bfloat16)

    token_sum = None
    for shift in range(n_head - 1, 0, -1):
        sent = term((me + shift) % n_head)
        pairs = [(i, (i + shift) % n_head) for i in range(n_head)]
        got = lax.ppermute(sent, "head", pairs).astype(jnp.float32)
        token_sum = got if token_sum is None else token_sum + got
    own = term(me).astype(jnp.float32)
    token_grad = (own if token_sum is None else token_sum + own).astype(jnp.bfloat16)
    proj_grads = jnp.concatenate([query_grad, key_grad, value_grad], axis=1)
    n_hi = lax.axis_size("seq_hi")
    core = lax.axis_index("core")
    swap = [(0, 1), (1, 0)]
    halves = gathered.reshape(tok_rows, n_hi, 2, -1)
    own_cols = lax.dynamic_index_in_dim(halves, core, 2, keepdims=False).reshape(tok_rows, -1)
    partner_cols = lax.dynamic_index_in_dim(halves, 1 - core, 2, keepdims=False).reshape(tok_rows, -1)
    partner_tokens = lax.ppermute(partner_cols, "core", swap)
    partner_grads = lax.ppermute(proj_grads, "core", swap)
    pair_tokens = jnp.concatenate([own_cols, partner_tokens], axis=0)
    pair_grads = jnp.concatenate([proj_grads, partner_grads], axis=0)
    pair_sum = contract_first(pair_grads, pair_tokens).astype(jnp.bfloat16)
    summed = lax.psum_scatter(pair_sum, "seq_hi", scatter_dimension=1, tiled=True)
    summed = summed.astype(jnp.float32)
    summed = (summed * (tok_rows * lax.axis_size(SEQ)) ** (-0.5)).astype(jnp.bfloat16).T
    q_width = query_weight.shape[1]
    k_width = key_weight.shape[1]
    query_weight_grad = summed[:, :q_width]
    key_weight_grad = summed[:, q_width : q_width + k_width]
    value_weight_grad = summed[:, q_width + k_width :]
    return (token_grad, query_weight_grad, key_weight_grad, value_weight_grad)


def solution(mesh):
    n_seq = mesh.shape["seq"]
    n_head = mesh.shape["head"]
    view = Mesh(mesh.devices.reshape(n_seq // 2, 2, n_head), ("seq_hi", "core", "head"))
    in_specs = (
        P(SEQ, "head"),
        P(None, "head"),
        P(None, "head"),
        P(None, "head"),
        P(SEQ, "head"),
        P(),
    )
    out_specs = (P(SEQ, "head"),) * 4
    return jax.shard_map(
        per_device, mesh=view, in_specs=in_specs, out_specs=out_specs, check_vma=False
    )
```

```python
import jax
import jax.numpy as jnp
from jax import lax
from jax.sharding import PartitionSpec as P

D = 5376
HEADS = 32
KV_HEADS = 16
HEAD_DIM = 128
WINDOW = 1024
HOPS = 2


neg_large = -1e30


def passed_along(x, axis, by):
    count = lax.axis_size(axis)
    pairs = [(i, i + by) for i in range(count) if 0 <= i + by < count]
    return lax.ppermute(x, axis, pairs)


def contract_last(left, right):
    return lax.dot_general(
        left, right, (((1,), (1,)), ((), ())), preferred_element_type=jnp.float32
    )


def contract_first(left, right):
    return lax.dot_general(
        left, right, (((0,), (0,)), ((), ())), preferred_element_type=jnp.float32
    )


def attend(queries, key_value, grads, query_first, key_first, seg_query, seg_key):
    tok_rows = queries.shape[0]
    key_rows = key_value.shape[1]
    groups = HEADS // KV_HEADS
    kv_local = key_value.shape[2] // HEAD_DIM
    score_scale = (D / HEADS) ** (-0.5)
    query_four = queries.reshape(tok_rows, kv_local, groups, HEAD_DIM)
    grad_four = grads.reshape(tok_rows, kv_local, groups, HEAD_DIM)
    key_three = key_value[0].reshape(key_rows, kv_local, HEAD_DIM)
    value_three = key_value[1].reshape(key_rows, kv_local, HEAD_DIM)
    query_pos = query_first + jnp.arange(tok_rows, dtype=jnp.int32)
    key_pos = key_first + jnp.arange(key_rows, dtype=jnp.int32)
    spacing = query_pos[:, None] - key_pos[None, :]
    allowed = (
        (key_pos >= 0)[None, :]
        & (spacing >= 0)
        & (spacing < WINDOW)
        & (seg_query[:, None] == seg_key[None, :])
    )
    scores = (
        jnp.einsum("akgd,ckd->kgac", query_four, key_three, preferred_element_type=jnp.float32)
        * score_scale
    )
    masked = jnp.where(allowed, scores, neg_large)
    row_max = jnp.max(masked, axis=-1, keepdims=True)
    expo = jnp.where(allowed, jnp.exp(masked - row_max), 0.0)
    probs = expo / jnp.sum(expo, axis=-1, keepdims=True)
    dprobs = jnp.einsum(
        "akgd,ckd->kgac", grad_four, value_three, preferred_element_type=jnp.float32
    )
    center = jnp.sum(probs * dprobs, axis=-1, keepdims=True)
    dscores = (probs * (dprobs - center)).astype(jnp.bfloat16)
    probs_low = probs.astype(jnp.bfloat16)
    query_grad = (
        (
            jnp.einsum("kgac,ckd->akgd", dscores, key_three, preferred_element_type=jnp.float32)
            * score_scale
        )
        .reshape(tok_rows, -1)
        .astype(jnp.bfloat16)
    )
    key_grad = (
        jnp.einsum("kgac,akgd->ckd", dscores, query_four, preferred_element_type=jnp.float32)
        * score_scale
    ).reshape(key_rows, -1)
    value_grad = jnp.einsum(
        "kgac,akgd->ckd", probs_low, grad_four, preferred_element_type=jnp.float32
    ).reshape(key_rows, -1)
    return (query_grad, jnp.stack([key_grad, value_grad]))


def per_device(tokens, query_weight, key_weight, value_weight, output_grad, segments):
    tok_rows = tokens.shape[0]
    hop_count = HOPS
    margin = hop_count * tok_rows
    gathered = lax.all_gather(tokens, "head", axis=1, tiled=True)
    position = lax.axis_index("seq")
    query_first = position * tok_rows
    seg_query = lax.dynamic_slice_in_dim(segments, query_first, tok_rows, 0)
    seg_padded = jnp.concatenate([jnp.full((margin,), -1, jnp.int32), segments], axis=0)
    seg_key = lax.dynamic_slice_in_dim(seg_padded, query_first, (hop_count + 1) * tok_rows, 0)
    n_seq = lax.axis_size("seq")
    weight_scale = (tok_rows * n_seq) ** (-0.5)
    kv_local = key_weight.shape[1] // HEAD_DIM
    n_split = 2 if kv_local % 2 == 0 else 1
    q_cols = query_weight.shape[1] // n_split
    k_cols = key_weight.shape[1] // n_split
    query_grads, key_grads, value_grads, reduced = [], [], [], []
    for part in range(n_split):
        wq = query_weight[:, part * q_cols : (part + 1) * q_cols]
        wk = key_weight[:, part * k_cols : (part + 1) * k_cols]
        wv = value_weight[:, part * k_cols : (part + 1) * k_cols]
        queries = jnp.dot(gathered, wq, preferred_element_type=jnp.float32).astype(jnp.bfloat16)
        keys_own = jnp.dot(gathered, wk, preferred_element_type=jnp.float32).astype(jnp.bfloat16)
        values_own = jnp.dot(gathered, wv, preferred_element_type=jnp.float32).astype(jnp.bfloat16)
        key_value = jnp.stack([keys_own, values_own])
        blocks = [key_value] * (hop_count + 1)
        for distance in range(1, hop_count + 1):
            blocks[hop_count - distance] = passed_along(key_value, "seq", distance)
        keys_all = jnp.concatenate(blocks, axis=1)
        grads = output_grad[:, part * q_cols : (part + 1) * q_cols]
        query_grad, kv_grad = attend(
            queries, keys_all, grads, query_first, query_first - margin, seg_query, seg_key
        )
        pieces = [
            kv_grad[:, block * tok_rows : (block + 1) * tok_rows]
            for block in range(hop_count + 1)
        ]
        carried = pieces[hop_count]
        for distance in range(1, hop_count + 1):
            back = passed_along(pieces[hop_count - distance].astype(jnp.bfloat16), "seq", -distance)
            carried = carried + back.astype(jnp.float32)
        key_grad = carried[0].astype(jnp.bfloat16)
        value_grad = carried[1].astype(jnp.bfloat16)
        proj_grads = jnp.concatenate([query_grad, key_grad, value_grad], axis=1)
        weight_part = contract_first(proj_grads, gathered).astype(jnp.bfloat16)
        reduced.append(lax.psum_scatter(weight_part, "seq", scatter_dimension=1, tiled=True))
        query_grads.append(query_grad)
        key_grads.append(key_grad)
        value_grads.append(value_grad)
    query_grad = jnp.concatenate(query_grads, axis=1)
    key_grad = jnp.concatenate(key_grads, axis=1)
    value_grad = jnp.concatenate(value_grads, axis=1)
    n_head = lax.axis_size("head")
    me = lax.axis_index("head")
    width = tokens.shape[1]

    def term(dest):
        start = dest * width
        part = contract_last(query_grad, lax.dynamic_slice_in_dim(query_weight, start, width, 0))
        part = part + contract_last(key_grad, lax.dynamic_slice_in_dim(key_weight, start, width, 0))
        part = part + contract_last(value_grad, lax.dynamic_slice_in_dim(value_weight, start, width, 0))
        return part.astype(jnp.bfloat16)

    token_sum = None
    for shift in range(n_head - 1, 0, -1):
        sent = term((me + shift) % n_head)
        pairs = [(i, (i + shift) % n_head) for i in range(n_head)]
        got = lax.ppermute(sent, "head", pairs).astype(jnp.float32)
        token_sum = got if token_sum is None else token_sum + got
    own = term(me).astype(jnp.float32)
    token_grad = (own if token_sum is None else token_sum + own).astype(jnp.bfloat16)

    def scaled(rows):
        return (rows.astype(jnp.float32) * weight_scale).astype(jnp.bfloat16).T

    query_weight_grad = jnp.concatenate([scaled(r[:q_cols]) for r in reduced], axis=1)
    key_weight_grad = jnp.concatenate([scaled(r[q_cols : q_cols + k_cols]) for r in reduced], axis=1)
    value_weight_grad = jnp.concatenate([scaled(r[q_cols + k_cols :]) for r in reduced], axis=1)
    return (token_grad, query_weight_grad, key_weight_grad, value_weight_grad)


def solution(mesh):
    in_specs = (
        P("seq", "head"),
        P(None, "head"),
        P(None, "head"),
        P(None, "head"),
        P("seq", "head"),
        P(),
    )
    out_specs = (P("seq", "head"), P("seq", "head"), P("seq", "head"), P("seq", "head"))
    return jax.shard_map(
        per_device, mesh=mesh, in_specs=in_specs, out_specs=out_specs, check_vma=False
    )
```

```python
import jax
import jax.numpy as jnp
from jax import lax
from jax.sharding import PartitionSpec as P

D = 5376
HEADS = 32
KV_HEADS = 16
HEAD_DIM = 128
WINDOW = 1024
HOPS = 2


neg_large = -1e30


def passed_along(x, axis, by):
    count = lax.axis_size(axis)
    pairs = [(i, i + by) for i in range(count) if 0 <= i + by < count]
    return lax.ppermute(x, axis, pairs)


def contract_last(left, right):
    return lax.dot_general(
        left, right, (((1,), (1,)), ((), ())), preferred_element_type=jnp.float32
    )


def contract_first(left, right):
    return lax.dot_general(
        left, right, (((0,), (0,)), ((), ())), preferred_element_type=jnp.float32
    )


def attend(queries, key_value, grads, query_first, key_first, seg_query, seg_key):
    tok_rows = queries.shape[0]
    key_rows = key_value.shape[1]
    groups = HEADS // KV_HEADS
    kv_local = key_value.shape[2] // HEAD_DIM
    score_scale = (D / HEADS) ** (-0.5)
    query_four = queries.reshape(tok_rows, kv_local, groups, HEAD_DIM)
    grad_four = grads.reshape(tok_rows, kv_local, groups, HEAD_DIM)
    key_three = key_value[0].reshape(key_rows, kv_local, HEAD_DIM)
    value_three = key_value[1].reshape(key_rows, kv_local, HEAD_DIM)
    query_pos = query_first + jnp.arange(tok_rows, dtype=jnp.int32)
    key_pos = key_first + jnp.arange(key_rows, dtype=jnp.int32)
    spacing = query_pos[:, None] - key_pos[None, :]
    allowed = (
        (key_pos >= 0)[None, :]
        & (spacing >= 0)
        & (spacing < WINDOW)
        & (seg_query[:, None] == seg_key[None, :])
    )
    scores = (
        jnp.einsum("akgd,ckd->kgac", query_four, key_three, preferred_element_type=jnp.float32)
        * score_scale
    )
    masked = jnp.where(allowed, scores, neg_large)
    row_max = jnp.max(masked, axis=-1, keepdims=True)
    expo = jnp.where(allowed, jnp.exp(masked - row_max), 0.0)
    probs = expo / jnp.sum(expo, axis=-1, keepdims=True)
    dprobs = jnp.einsum(
        "akgd,ckd->kgac", grad_four, value_three, preferred_element_type=jnp.float32
    )
    center = jnp.sum(probs * dprobs, axis=-1, keepdims=True)
    dscores = (probs * (dprobs - center)).astype(jnp.bfloat16)
    probs_low = probs.astype(jnp.bfloat16)
    query_grad = (
        (
            jnp.einsum("kgac,ckd->akgd", dscores, key_three, preferred_element_type=jnp.float32)
            * score_scale
        )
        .reshape(tok_rows, -1)
        .astype(jnp.bfloat16)
    )
    key_grad = (
        jnp.einsum("kgac,akgd->ckd", dscores, query_four, preferred_element_type=jnp.float32)
        * score_scale
    ).reshape(key_rows, -1)
    value_grad = jnp.einsum(
        "kgac,akgd->ckd", probs_low, grad_four, preferred_element_type=jnp.float32
    ).reshape(key_rows, -1)
    return (query_grad, jnp.stack([key_grad, value_grad]))


def per_device(tokens, query_weight, key_weight, value_weight, output_grad, segments):
    tok_rows = tokens.shape[0]
    hop_count = HOPS
    margin = hop_count * tok_rows
    gathered = lax.all_gather(tokens, "head", axis=1, tiled=True)
    queries = jnp.dot(gathered, query_weight, preferred_element_type=jnp.float32).astype(
        jnp.bfloat16
    )
    keys_own = jnp.dot(gathered, key_weight, preferred_element_type=jnp.float32).astype(
        jnp.bfloat16
    )
    values_own = jnp.dot(gathered, value_weight, preferred_element_type=jnp.float32).astype(
        jnp.bfloat16
    )
    key_value = jnp.stack([keys_own, values_own])
    blocks = [key_value] * (hop_count + 1)
    moving = key_value
    for distance in range(1, hop_count + 1):
        moving = passed_along(moving, "seq", 1)
        blocks[hop_count - distance] = moving
    keys_all = jnp.concatenate(blocks, axis=1)
    position = lax.axis_index("seq")
    query_first = position * tok_rows
    seg_query = lax.dynamic_slice_in_dim(segments, query_first, tok_rows, 0)
    seg_padded = jnp.concatenate([jnp.full((margin,), -1, jnp.int32), segments], axis=0)
    seg_key = lax.dynamic_slice_in_dim(seg_padded, query_first, (hop_count + 1) * tok_rows, 0)
    query_grad, kv_grad = attend(
        queries, keys_all, output_grad, query_first, query_first - margin, seg_query, seg_key
    )
    pieces = [
        kv_grad[:, block * tok_rows : (block + 1) * tok_rows] for block in range(hop_count + 1)
    ]
    carried = pieces[0]
    for distance in range(1, hop_count + 1):
        carried = pieces[distance] + passed_along(carried.astype(jnp.bfloat16), "seq", -1).astype(
            carried.dtype
        )
    key_grad = carried[0].astype(jnp.bfloat16)
    value_grad = carried[1].astype(jnp.bfloat16)
    n_head = lax.axis_size("head")
    me = lax.axis_index("head")
    width = tokens.shape[1]
    q_part = contract_first(query_grad, gathered).astype(jnp.bfloat16)
    q_reduced = lax.psum_scatter(q_part, "seq", scatter_dimension=1, tiled=True)
    kv_part = contract_first(
        jnp.concatenate([key_grad, value_grad], axis=1), gathered
    ).astype(jnp.bfloat16)
    kv_reduced = lax.psum_scatter(kv_part, "seq", scatter_dimension=1, tiled=True)
    partial_term = (
        contract_last(query_grad, query_weight)
        + contract_last(key_grad, key_weight)
        + contract_last(value_grad, value_weight)
    )

    def block_of(dest):
        return lax.dynamic_slice_in_dim(partial_term, dest * width, width, 1)

    from_left = None
    from_right = None
    for step in range(1, n_head):
        gap = n_head - step
        rightward = block_of(jnp.minimum(me + gap, n_head - 1))
        if from_left is not None:
            rightward = rightward + from_left.astype(jnp.float32)
        right_pairs = [(h, h + 1) for h in range(min(step, n_head - 1))]
        from_left = lax.ppermute(rightward.astype(jnp.bfloat16), "head", right_pairs)
        leftward = block_of(jnp.maximum(me - gap, 0))
        if from_right is not None:
            leftward = leftward + from_right.astype(jnp.float32)
        left_pairs = [(h, h - 1) for h in range(max(gap, 1), n_head)]
        from_right = lax.ppermute(leftward.astype(jnp.bfloat16), "head", left_pairs)
    token_sum = block_of(me)
    if from_left is not None:
        token_sum = token_sum + from_left.astype(jnp.float32) + from_right.astype(jnp.float32)
    token_grad = token_sum.astype(jnp.bfloat16)
    weight_scale = (tok_rows * lax.axis_size("seq")) ** (-0.5)

    def scaled(rows):
        return (rows.astype(jnp.float32) * weight_scale).astype(jnp.bfloat16).T

    k_width = key_weight.shape[1]
    query_weight_grad = scaled(q_reduced)
    key_weight_grad = scaled(kv_reduced[:k_width])
    value_weight_grad = scaled(kv_reduced[k_width:])
    return (token_grad, query_weight_grad, key_weight_grad, value_weight_grad)


def solution(mesh):
    in_specs = (
        P("seq", "head"),
        P(None, "head"),
        P(None, "head"),
        P(None, "head"),
        P("seq", "head"),
        P(),
    )
    out_specs = (P("seq", "head"), P("seq", "head"), P("seq", "head"), P("seq", "head"))
    return jax.shard_map(
        per_device, mesh=mesh, in_specs=in_specs, out_specs=out_specs, check_vma=False
    )
```

```python
import jax
import jax.numpy as jnp
from jax import lax
from jax.sharding import Mesh, PartitionSpec as P

D = 5376
HEADS = 32
KV_HEADS = 16
HEAD_DIM = 128
WINDOW = 1024
HOPS = 2
SEQ = ("seq_hi", "core")


neg_large = -1e30


def passed_along(x, axis, by):
    count = lax.axis_size(axis)
    pairs = [(i, i + by) for i in range(count) if 0 <= i + by < count]
    return lax.ppermute(x, axis, pairs)


def contract_last(left, right):
    return lax.dot_general(
        left, right, (((1,), (1,)), ((), ())), preferred_element_type=jnp.float32
    )


def contract_first(left, right):
    return lax.dot_general(
        left, right, (((0,), (0,)), ((), ())), preferred_element_type=jnp.float32
    )


def attend(queries, key_value, grads, query_first, key_first, seg_query, seg_key):
    tok_rows = queries.shape[0]
    key_rows = key_value.shape[1]
    groups = HEADS // KV_HEADS
    kv_local = key_value.shape[2] // HEAD_DIM
    score_scale = (D / HEADS) ** (-0.5)
    query_four = queries.reshape(tok_rows, kv_local, groups, HEAD_DIM)
    grad_four = grads.reshape(tok_rows, kv_local, groups, HEAD_DIM)
    key_three = key_value[0].reshape(key_rows, kv_local, HEAD_DIM)
    value_three = key_value[1].reshape(key_rows, kv_local, HEAD_DIM)
    query_pos = query_first + jnp.arange(tok_rows, dtype=jnp.int32)
    key_pos = key_first + jnp.arange(key_rows, dtype=jnp.int32)
    spacing = query_pos[:, None] - key_pos[None, :]
    allowed = (
        (key_pos >= 0)[None, :]
        & (spacing >= 0)
        & (spacing < WINDOW)
        & (seg_query[:, None] == seg_key[None, :])
    )
    scores = (
        jnp.einsum("akgd,ckd->kgac", query_four, key_three, preferred_element_type=jnp.float32)
        * score_scale
    )
    masked = jnp.where(allowed, scores, neg_large)
    row_max = jnp.max(masked, axis=-1, keepdims=True)
    expo = jnp.where(allowed, jnp.exp(masked - row_max), 0.0)
    probs = expo / jnp.sum(expo, axis=-1, keepdims=True)
    dprobs = jnp.einsum(
        "akgd,ckd->kgac", grad_four, value_three, preferred_element_type=jnp.float32
    )
    center = jnp.sum(probs * dprobs, axis=-1, keepdims=True)
    dscores = (probs * (dprobs - center)).astype(jnp.bfloat16)
    probs_low = probs.astype(jnp.bfloat16)
    query_grad = (
        (
            jnp.einsum("kgac,ckd->akgd", dscores, key_three, preferred_element_type=jnp.float32)
            * score_scale
        )
        .reshape(tok_rows, -1)
        .astype(jnp.bfloat16)
    )
    key_grad = (
        jnp.einsum("kgac,akgd->ckd", dscores, query_four, preferred_element_type=jnp.float32)
        * score_scale
    ).reshape(key_rows, -1)
    value_grad = jnp.einsum(
        "kgac,akgd->ckd", probs_low, grad_four, preferred_element_type=jnp.float32
    ).reshape(key_rows, -1)
    return (query_grad, jnp.stack([key_grad, value_grad]))


def per_device(tokens, query_weight, key_weight, value_weight, output_grad, segments):
    tok_rows = tokens.shape[0]
    hop_count = HOPS
    margin = hop_count * tok_rows
    gathered = lax.all_gather(tokens, "head", axis=1, tiled=True)
    queries = jnp.dot(gathered, query_weight, preferred_element_type=jnp.float32).astype(
        jnp.bfloat16
    )
    keys_own = jnp.dot(gathered, key_weight, preferred_element_type=jnp.float32).astype(
        jnp.bfloat16
    )
    values_own = jnp.dot(gathered, value_weight, preferred_element_type=jnp.float32).astype(
        jnp.bfloat16
    )
    key_value = jnp.stack([keys_own, values_own])
    blocks = [key_value] * (hop_count + 1)
    for distance in range(1, hop_count + 1):
        blocks[hop_count - distance] = passed_along(key_value, SEQ, distance)
    keys_all = jnp.concatenate(blocks, axis=1)
    position = lax.axis_index(SEQ)
    query_first = position * tok_rows
    seg_query = lax.dynamic_slice_in_dim(segments, query_first, tok_rows, 0)
    seg_padded = jnp.concatenate([jnp.full((margin,), -1, jnp.int32), segments], axis=0)
    seg_key = lax.dynamic_slice_in_dim(seg_padded, query_first, (hop_count + 1) * tok_rows, 0)
    query_grad, kv_grad = attend(
        queries, keys_all, output_grad, query_first, query_first - margin, seg_query, seg_key
    )
    pieces = [
        kv_grad[:, block * tok_rows : (block + 1) * tok_rows] for block in range(hop_count + 1)
    ]
    carried = pieces[hop_count]
    for distance in range(1, hop_count + 1):
        back = passed_along(pieces[hop_count - distance].astype(jnp.bfloat16), SEQ, -distance)
        carried = carried + back.astype(jnp.float32)
    key_grad = carried[0].astype(jnp.bfloat16)
    value_grad = carried[1].astype(jnp.bfloat16)
    n_head = lax.axis_size("head")
    me = lax.axis_index("head")
    width = tokens.shape[1]

    def term(dest):
        start = dest * width
        part = contract_last(query_grad, lax.dynamic_slice_in_dim(query_weight, start, width, 0))
        part = part + contract_last(key_grad, lax.dynamic_slice_in_dim(key_weight, start, width, 0))
        part = part + contract_last(value_grad, lax.dynamic_slice_in_dim(value_weight, start, width, 0))
        return part.astype(jnp.bfloat16)

    token_sum = None
    outgoing = []
    for shift in range(n_head - 1, 0, -1):
        sent = term((me + shift) % n_head)
        outgoing.append(sent)
        pairs = [(i, (i + shift) % n_head) for i in range(n_head)]
        got = lax.ppermute(sent, "head", pairs).astype(jnp.float32)
        token_sum = got if token_sum is None else token_sum + got
    own = term(me).astype(jnp.float32)
    token_grad = (own if token_sum is None else token_sum + own).astype(jnp.bfloat16)
    proj_grads = jnp.concatenate([query_grad, key_grad, value_grad], axis=1)
    proj_grads, _ = lax.optimization_barrier((proj_grads, outgoing))
    n_hi = lax.axis_size("seq_hi")
    core = lax.axis_index("core")
    swap = [(0, 1), (1, 0)]
    halves = gathered.reshape(tok_rows, n_hi, 2, -1)
    own_cols = lax.dynamic_index_in_dim(halves, core, 2, keepdims=False).reshape(tok_rows, -1)
    partner_cols = lax.dynamic_index_in_dim(halves, 1 - core, 2, keepdims=False).reshape(tok_rows, -1)
    both_halves = lax.all_gather(partner_cols, "core", axis=0, tiled=True)
    partner_tokens = lax.dynamic_slice_in_dim(both_halves, (1 - core) * tok_rows, tok_rows, 0)
    first = jnp.where(core == 0, own_cols, partner_tokens)
    second = jnp.where(core == 0, partner_tokens, own_cols)
    pair_tokens = jnp.concatenate([first, second], axis=0)
    pair_grads = lax.all_gather(proj_grads, "core", axis=0, tiled=True)
    pair_sum = contract_first(pair_grads, pair_tokens).astype(jnp.bfloat16)
    summed = lax.psum_scatter(pair_sum, "seq_hi", scatter_dimension=1, tiled=True)
    summed = summed.astype(jnp.float32)
    summed = (summed * (tok_rows * lax.axis_size(SEQ)) ** (-0.5)).astype(jnp.bfloat16).T
    q_width = query_weight.shape[1]
    k_width = key_weight.shape[1]
    query_weight_grad = summed[:, :q_width]
    key_weight_grad = summed[:, q_width : q_width + k_width]
    value_weight_grad = summed[:, q_width + k_width :]
    return (token_grad, query_weight_grad, key_weight_grad, value_weight_grad)


def solution(mesh):
    n_seq = mesh.shape["seq"]
    n_head = mesh.shape["head"]
    view = Mesh(mesh.devices.reshape(n_seq // 2, 2, n_head), ("seq_hi", "core", "head"))
    in_specs = (
        P(SEQ, "head"),
        P(None, "head"),
        P(None, "head"),
        P(None, "head"),
        P(SEQ, "head"),
        P(),
    )
    out_specs = (P(SEQ, "head"),) * 4
    return jax.shard_map(
        per_device, mesh=view, in_specs=in_specs, out_specs=out_specs, check_vma=False
    )
```

```python
import jax
import jax.numpy as jnp
from jax import lax
from jax.experimental import pallas as pl
from jax.experimental.pallas import tpu as pltpu
from jax.sharding import PartitionSpec as P

D = 5376
HEADS = 32
KV_HEADS = 16
HEAD_DIM = 128
WINDOW = 1024
HOPS = 2


neg_large = -1e30


def passed_along(x, axis, by):
    count = lax.axis_size(axis)
    pairs = [(i, i + by) for i in range(count) if 0 <= i + by < count]
    return lax.ppermute(x, axis, pairs)


def contract_last(left, right):
    return lax.dot_general(
        left, right, (((1,), (1,)), ((), ())), preferred_element_type=jnp.float32
    )


def contract_first(left, right):
    return lax.dot_general(
        left, right, (((0,), (0,)), ((), ())), preferred_element_type=jnp.float32
    )


def attention_kernel(mask_ref, q_ref, k_ref, v_ref, g_ref, qg_ref, kg_ref, vg_ref):
    score_scale = (D / HEADS) ** (-0.5)
    rows = mask_ref.shape[0]
    groups = q_ref.shape[1] // rows
    allowed = mask_ref[...] > 0.5
    keys = k_ref[0]
    values = v_ref[0]
    key_acc = jnp.zeros(kg_ref.shape[1:], jnp.float32)
    value_acc = jnp.zeros(vg_ref.shape[1:], jnp.float32)
    for group in range(groups):
        rows_of = slice(group * rows, (group + 1) * rows)
        queries = q_ref[0, rows_of, :]
        grads = g_ref[0, rows_of, :]
        scores = contract_last(queries, keys) * score_scale
        masked = jnp.where(allowed, scores, neg_large)
        row_max = jnp.max(masked, axis=-1, keepdims=True)
        expo = jnp.where(allowed, jnp.exp(masked - row_max), 0.0)
        probs = expo / jnp.sum(expo, axis=-1, keepdims=True)
        dprobs = contract_last(grads, values)
        center = jnp.sum(probs * dprobs, axis=-1, keepdims=True)
        dscores = (probs * (dprobs - center)).astype(jnp.bfloat16)
        probs_low = probs.astype(jnp.bfloat16)
        query_grad = jnp.dot(dscores, keys, preferred_element_type=jnp.float32) * score_scale
        qg_ref[0, rows_of, :] = query_grad.astype(jnp.bfloat16)
        key_acc = key_acc + contract_first(dscores, queries)
        value_acc = value_acc + contract_first(probs_low, grads)
    kg_ref[0] = key_acc * score_scale
    vg_ref[0] = value_acc


def attend(queries, key_value, grads, query_first, key_first, seg_query, seg_key):
    tok_rows = queries.shape[0]
    key_rows = key_value.shape[1]
    groups = HEADS // KV_HEADS
    kv_local = key_value.shape[2] // HEAD_DIM
    query_pos = query_first + jnp.arange(tok_rows, dtype=jnp.int32)
    key_pos = key_first + jnp.arange(key_rows, dtype=jnp.int32)
    spacing = query_pos[:, None] - key_pos[None, :]
    allowed = (
        (key_pos >= 0)[None, :]
        & (spacing >= 0)
        & (spacing < WINDOW)
        & (seg_query[:, None] == seg_key[None, :])
    )
    mask = allowed.astype(jnp.float32)

    def by_head(x, rows):
        return x.reshape(rows, kv_local, -1, HEAD_DIM).transpose(1, 2, 0, 3).reshape(kv_local, -1, HEAD_DIM)

    q_heads = by_head(queries, tok_rows)
    g_heads = by_head(grads, tok_rows)
    k_heads = by_head(key_value[0], key_rows)
    v_heads = by_head(key_value[1], key_rows)
    q_spec = pl.BlockSpec((1, groups * tok_rows, HEAD_DIM), lambda h: (h, 0, 0))
    k_spec = pl.BlockSpec((1, key_rows, HEAD_DIM), lambda h: (h, 0, 0))
    q_grad, k_grad, v_grad = pl.pallas_call(
        attention_kernel,
        grid=(kv_local,),
        in_specs=[
            pl.BlockSpec((tok_rows, key_rows), lambda h: (0, 0)),
            q_spec,
            k_spec,
            k_spec,
            q_spec,
        ],
        out_specs=[q_spec, k_spec, k_spec],
        out_shape=[
            jax.ShapeDtypeStruct(q_heads.shape, jnp.bfloat16),
            jax.ShapeDtypeStruct(k_heads.shape, jnp.float32),
            jax.ShapeDtypeStruct(k_heads.shape, jnp.float32),
        ],
        compiler_params=pltpu.CompilerParams(vmem_limit_bytes=56 * 1024 * 1024),
    )(mask, q_heads, k_heads, v_heads, g_heads)
    query_grad = (
        q_grad.reshape(kv_local, groups, tok_rows, HEAD_DIM)
        .transpose(2, 0, 1, 3)
        .reshape(tok_rows, -1)
    )

    def by_row(x):
        return x.transpose(1, 0, 2).reshape(key_rows, -1)

    return (query_grad, jnp.stack([by_row(k_grad), by_row(v_grad)]))


def per_device(tokens, query_weight, key_weight, value_weight, output_grad, segments):
    tok_rows = tokens.shape[0]
    hop_count = HOPS
    margin = hop_count * tok_rows
    gathered = lax.all_gather(tokens, "head", axis=1, tiled=True)
    queries = jnp.dot(gathered, query_weight, preferred_element_type=jnp.float32).astype(
        jnp.bfloat16
    )
    keys_own = jnp.dot(gathered, key_weight, preferred_element_type=jnp.float32).astype(
        jnp.bfloat16
    )
    values_own = jnp.dot(gathered, value_weight, preferred_element_type=jnp.float32).astype(
        jnp.bfloat16
    )
    key_value = jnp.stack([keys_own, values_own])
    blocks = [key_value] * (hop_count + 1)
    moving = key_value
    for distance in range(1, hop_count + 1):
        moving = passed_along(moving, "seq", 1)
        blocks[hop_count - distance] = moving
    keys_all = jnp.concatenate(blocks, axis=1)
    position = lax.axis_index("seq")
    query_first = position * tok_rows
    seg_query = lax.dynamic_slice_in_dim(segments, query_first, tok_rows, 0)
    seg_padded = jnp.concatenate([jnp.full((margin,), -1, jnp.int32), segments], axis=0)
    seg_key = lax.dynamic_slice_in_dim(seg_padded, query_first, (hop_count + 1) * tok_rows, 0)
    query_grad, kv_grad = attend(
        queries, keys_all, output_grad, query_first, query_first - margin, seg_query, seg_key
    )
    pieces = [
        kv_grad[:, block * tok_rows : (block + 1) * tok_rows] for block in range(hop_count + 1)
    ]
    carried = pieces[0]
    for distance in range(1, hop_count + 1):
        carried = pieces[distance] + passed_along(carried.astype(jnp.bfloat16), "seq", -1).astype(
            carried.dtype
        )
    key_grad = carried[0].astype(jnp.bfloat16)
    value_grad = carried[1].astype(jnp.bfloat16)
    n_head = lax.axis_size("head")
    me = lax.axis_index("head")
    width = tokens.shape[1]

    def term(dest):
        start = dest * width
        part = contract_last(query_grad, lax.dynamic_slice_in_dim(query_weight, start, width, 0))
        part = part + contract_last(key_grad, lax.dynamic_slice_in_dim(key_weight, start, width, 0))
        part = part + contract_last(value_grad, lax.dynamic_slice_in_dim(value_weight, start, width, 0))
        return part.astype(jnp.bfloat16)

    token_sum = None
    for shift in range(n_head - 1, 0, -1):
        sent = term((me + shift) % n_head)
        pairs = [(i, (i + shift) % n_head) for i in range(n_head)]
        got = lax.ppermute(sent, "head", pairs).astype(jnp.float32)
        token_sum = got if token_sum is None else token_sum + got
    own = term(me).astype(jnp.float32)
    token_grad = (own if token_sum is None else token_sum + own).astype(jnp.bfloat16)
    proj_grads = jnp.concatenate([query_grad, key_grad, value_grad], axis=1)
    summed = lax.psum_scatter(
        contract_first(proj_grads, gathered).astype(jnp.bfloat16),
        "seq",
        scatter_dimension=1,
        tiled=True,
    ).astype(jnp.float32)
    summed = (summed * (tok_rows * lax.axis_size("seq")) ** (-0.5)).astype(jnp.bfloat16).T
    q_width = query_weight.shape[1]
    k_width = key_weight.shape[1]
    query_weight_grad = summed[:, :q_width]
    key_weight_grad = summed[:, q_width : q_width + k_width]
    value_weight_grad = summed[:, q_width + k_width :]
    return (token_grad, query_weight_grad, key_weight_grad, value_weight_grad)


def solution(mesh):
    in_specs = (
        P("seq", "head"),
        P(None, "head"),
        P(None, "head"),
        P(None, "head"),
        P("seq", "head"),
        P(),
    )
    out_specs = (P("seq", "head"), P("seq", "head"), P("seq", "head"), P("seq", "head"))
    return jax.shard_map(
        per_device, mesh=mesh, in_specs=in_specs, out_specs=out_specs, check_vma=False
    )
```

```python
import jax
import jax.numpy as jnp
from jax import lax
from jax.experimental import pallas as pl
from jax.experimental.pallas import tpu as pltpu
from jax.sharding import PartitionSpec as P

D = 5376
HEADS = 32
KV_HEADS = 16
HEAD_DIM = 128
WINDOW = 1024
HOPS = 2


neg_large = -1e30


def passed_along(x, axis, by):
    count = lax.axis_size(axis)
    pairs = [(i, i + by) for i in range(count) if 0 <= i + by < count]
    return lax.ppermute(x, axis, pairs)


def contract_last(left, right):
    return lax.dot_general(
        left, right, (((1,), (1,)), ((), ())), preferred_element_type=jnp.float32
    )


def contract_first(left, right):
    return lax.dot_general(
        left, right, (((0,), (0,)), ((), ())), preferred_element_type=jnp.float32
    )


def attention_kernel(mask_ref, q_ref, k_ref, v_ref, g_ref, qg_ref, kg_ref, vg_ref):
    score_scale = (D / HEADS) ** (-0.5)
    groups = q_ref.shape[1] // HEAD_DIM
    allowed = mask_ref[...] > 0.5
    keys = k_ref[0]
    values = v_ref[0]
    key_acc = jnp.zeros(kg_ref.shape, jnp.float32)
    value_acc = jnp.zeros(vg_ref.shape, jnp.float32)
    for group in range(groups):
        cols = slice(group * HEAD_DIM, (group + 1) * HEAD_DIM)
        queries = q_ref[:, cols]
        grads = g_ref[:, cols]
        scores = contract_last(queries, keys) * score_scale
        masked = jnp.where(allowed, scores, neg_large)
        row_max = jnp.max(masked, axis=-1, keepdims=True)
        expo = jnp.where(allowed, jnp.exp(masked - row_max), 0.0)
        probs = expo / jnp.sum(expo, axis=-1, keepdims=True)
        dprobs = contract_last(grads, values)
        center = jnp.sum(probs * dprobs, axis=-1, keepdims=True)
        dscores = (probs * (dprobs - center)).astype(jnp.bfloat16)
        probs_low = probs.astype(jnp.bfloat16)
        query_grad = jnp.dot(dscores, keys, preferred_element_type=jnp.float32) * score_scale
        qg_ref[:, cols] = query_grad.astype(jnp.bfloat16)
        key_acc = key_acc + contract_first(dscores, queries)
        value_acc = value_acc + contract_first(probs_low, grads)
    kg_ref[...] = key_acc * score_scale
    vg_ref[...] = value_acc


def attend(queries, key_value, grads, query_first, key_first, seg_query, seg_key):
    tok_rows = queries.shape[0]
    key_rows = key_value.shape[1]
    groups = HEADS // KV_HEADS
    kv_local = key_value.shape[2] // HEAD_DIM
    query_pos = query_first + jnp.arange(tok_rows, dtype=jnp.int32)
    key_pos = key_first + jnp.arange(key_rows, dtype=jnp.int32)
    spacing = query_pos[:, None] - key_pos[None, :]
    allowed = (
        (key_pos >= 0)[None, :]
        & (spacing >= 0)
        & (spacing < WINDOW)
        & (seg_query[:, None] == seg_key[None, :])
    )
    mask = allowed.astype(jnp.float32)
    q_spec = pl.BlockSpec((tok_rows, groups * HEAD_DIM), lambda h: (0, h))
    kv_out_spec = pl.BlockSpec((key_rows, HEAD_DIM), lambda h: (0, h))
    query_grad, key_grad, value_grad = pl.pallas_call(
        attention_kernel,
        grid=(kv_local,),
        in_specs=[
            pl.BlockSpec((tok_rows, key_rows), lambda h: (0, 0)),
            q_spec,
            pl.BlockSpec((1, key_rows, HEAD_DIM), lambda h: (0, 0, h)),
            pl.BlockSpec((1, key_rows, HEAD_DIM), lambda h: (1, 0, h)),
            q_spec,
        ],
        out_specs=[q_spec, kv_out_spec, kv_out_spec],
        out_shape=[
            jax.ShapeDtypeStruct(queries.shape, jnp.bfloat16),
            jax.ShapeDtypeStruct(key_value.shape[1:], jnp.float32),
            jax.ShapeDtypeStruct(key_value.shape[1:], jnp.float32),
        ],
        compiler_params=pltpu.CompilerParams(vmem_limit_bytes=56 * 1024 * 1024),
    )(mask, queries, key_value, key_value, grads)
    return (query_grad, jnp.stack([key_grad, value_grad]))


def per_device(tokens, query_weight, key_weight, value_weight, output_grad, segments):
    tok_rows = tokens.shape[0]
    hop_count = HOPS
    margin = hop_count * tok_rows
    gathered = lax.all_gather(tokens, "head", axis=1, tiled=True)
    queries = jnp.dot(gathered, query_weight, preferred_element_type=jnp.float32).astype(
        jnp.bfloat16
    )
    keys_own = jnp.dot(gathered, key_weight, preferred_element_type=jnp.float32).astype(
        jnp.bfloat16
    )
    values_own = jnp.dot(gathered, value_weight, preferred_element_type=jnp.float32).astype(
        jnp.bfloat16
    )
    key_value = jnp.stack([keys_own, values_own])
    blocks = [key_value] * (hop_count + 1)
    moving = key_value
    for distance in range(1, hop_count + 1):
        moving = passed_along(moving, "seq", 1)
        blocks[hop_count - distance] = moving
    keys_all = jnp.concatenate(blocks, axis=1)
    position = lax.axis_index("seq")
    query_first = position * tok_rows
    seg_query = lax.dynamic_slice_in_dim(segments, query_first, tok_rows, 0)
    seg_padded = jnp.concatenate([jnp.full((margin,), -1, jnp.int32), segments], axis=0)
    seg_key = lax.dynamic_slice_in_dim(seg_padded, query_first, (hop_count + 1) * tok_rows, 0)
    query_grad, kv_grad = attend(
        queries, keys_all, output_grad, query_first, query_first - margin, seg_query, seg_key
    )
    pieces = [
        kv_grad[:, block * tok_rows : (block + 1) * tok_rows] for block in range(hop_count + 1)
    ]
    carried = pieces[0]
    for distance in range(1, hop_count + 1):
        carried = pieces[distance] + passed_along(carried.astype(jnp.bfloat16), "seq", -1).astype(
            carried.dtype
        )
    key_grad = carried[0].astype(jnp.bfloat16)
    value_grad = carried[1].astype(jnp.bfloat16)
    n_head = lax.axis_size("head")
    me = lax.axis_index("head")
    width = tokens.shape[1]

    def term(dest):
        start = dest * width
        part = contract_last(query_grad, lax.dynamic_slice_in_dim(query_weight, start, width, 0))
        part = part + contract_last(key_grad, lax.dynamic_slice_in_dim(key_weight, start, width, 0))
        part = part + contract_last(value_grad, lax.dynamic_slice_in_dim(value_weight, start, width, 0))
        return part.astype(jnp.bfloat16)

    token_sum = None
    for shift in range(n_head - 1, 0, -1):
        sent = term((me + shift) % n_head)
        pairs = [(i, (i + shift) % n_head) for i in range(n_head)]
        got = lax.ppermute(sent, "head", pairs).astype(jnp.float32)
        token_sum = got if token_sum is None else token_sum + got
    own = term(me).astype(jnp.float32)
    token_grad = (own if token_sum is None else token_sum + own).astype(jnp.bfloat16)
    proj_grads = jnp.concatenate([query_grad, key_grad, value_grad], axis=1)
    summed = lax.psum_scatter(
        contract_first(proj_grads, gathered).astype(jnp.bfloat16),
        "seq",
        scatter_dimension=1,
        tiled=True,
    ).astype(jnp.float32)
    summed = (summed * (tok_rows * lax.axis_size("seq")) ** (-0.5)).astype(jnp.bfloat16).T
    q_width = query_weight.shape[1]
    k_width = key_weight.shape[1]
    query_weight_grad = summed[:, :q_width]
    key_weight_grad = summed[:, q_width : q_width + k_width]
    value_weight_grad = summed[:, q_width + k_width :]
    return (token_grad, query_weight_grad, key_weight_grad, value_weight_grad)


def solution(mesh):
    in_specs = (
        P("seq", "head"),
        P(None, "head"),
        P(None, "head"),
        P(None, "head"),
        P("seq", "head"),
        P(),
    )
    out_specs = (P("seq", "head"), P("seq", "head"), P("seq", "head"), P("seq", "head"))
    return jax.shard_map(
        per_device, mesh=mesh, in_specs=in_specs, out_specs=out_specs, check_vma=False
    )
```

```python
import jax
import jax.numpy as jnp
from jax import lax
from jax.experimental import pallas as pl
from jax.experimental.pallas import tpu as pltpu
from jax.sharding import PartitionSpec as P

D = 5376
HEADS = 32
KV_HEADS = 16
HEAD_DIM = 128
WINDOW = 1024
HOPS = 2


neg_large = -1e30


def passed_along(x, axis, by):
    count = lax.axis_size(axis)
    pairs = [(i, i + by) for i in range(count) if 0 <= i + by < count]
    return lax.ppermute(x, axis, pairs)


def contract_last(left, right):
    return lax.dot_general(
        left, right, (((1,), (1,)), ((), ())), preferred_element_type=jnp.float32
    )


def contract_first(left, right):
    return lax.dot_general(
        left, right, (((0,), (0,)), ((), ())), preferred_element_type=jnp.float32
    )


def attention_kernel(mask_ref, q_ref, k_ref, v_ref, g_ref, qg_ref, kg_ref, vg_ref):
    score_scale = (D / HEADS) ** (-0.5)
    groups = q_ref.shape[1] // HEAD_DIM
    allowed = mask_ref[...] > 0.5
    keys = k_ref[0]
    values = v_ref[0]
    key_acc = jnp.zeros(kg_ref.shape, jnp.float32)
    value_acc = jnp.zeros(vg_ref.shape, jnp.float32)
    for group in range(groups):
        cols = slice(group * HEAD_DIM, (group + 1) * HEAD_DIM)
        queries = q_ref[:, cols]
        grads = g_ref[:, cols]
        scores = contract_last(queries, keys) * score_scale
        masked = jnp.where(allowed, scores, neg_large)
        row_max = jnp.max(masked, axis=-1, keepdims=True)
        expo = jnp.where(allowed, jnp.exp(masked - row_max), 0.0)
        probs = expo / jnp.sum(expo, axis=-1, keepdims=True)
        dprobs = contract_last(grads, values)
        center = jnp.sum(probs * dprobs, axis=-1, keepdims=True)
        dscores = (probs * (dprobs - center)).astype(jnp.bfloat16)
        probs_low = probs.astype(jnp.bfloat16)
        query_grad = jnp.dot(dscores, keys, preferred_element_type=jnp.float32) * score_scale
        qg_ref[:, cols] = query_grad.astype(jnp.bfloat16)
        key_acc = key_acc + contract_first(dscores, queries)
        value_acc = value_acc + contract_first(probs_low, grads)
    kg_ref[...] = key_acc * score_scale
    vg_ref[...] = value_acc


def attend(queries, key_value, grads, query_first, key_first, seg_query, seg_key):
    tok_rows = queries.shape[0]
    key_rows = key_value.shape[1]
    groups = HEADS // KV_HEADS
    kv_local = key_value.shape[2] // HEAD_DIM
    query_pos = query_first + jnp.arange(tok_rows, dtype=jnp.int32)
    key_pos = key_first + jnp.arange(key_rows, dtype=jnp.int32)
    spacing = query_pos[:, None] - key_pos[None, :]
    allowed = (
        (key_pos >= 0)[None, :]
        & (spacing >= 0)
        & (spacing < WINDOW)
        & (seg_query[:, None] == seg_key[None, :])
    )
    mask = allowed.astype(jnp.float32)
    q_spec = pl.BlockSpec((tok_rows, groups * HEAD_DIM), lambda h: (0, h))
    kv_out_spec = pl.BlockSpec((key_rows, HEAD_DIM), lambda h: (0, h))
    query_grad, key_grad, value_grad = pl.pallas_call(
        attention_kernel,
        grid=(kv_local,),
        in_specs=[
            pl.BlockSpec((tok_rows, key_rows), lambda h: (0, 0)),
            q_spec,
            pl.BlockSpec((1, key_rows, HEAD_DIM), lambda h: (0, 0, h)),
            pl.BlockSpec((1, key_rows, HEAD_DIM), lambda h: (1, 0, h)),
            q_spec,
        ],
        out_specs=[q_spec, kv_out_spec, kv_out_spec],
        out_shape=[
            jax.ShapeDtypeStruct(queries.shape, jnp.bfloat16),
            jax.ShapeDtypeStruct(key_value.shape[1:], jnp.float32),
            jax.ShapeDtypeStruct(key_value.shape[1:], jnp.float32),
        ],
        compiler_params=pltpu.CompilerParams(vmem_limit_bytes=56 * 1024 * 1024),
    )(mask, queries, key_value, key_value, grads)
    return (query_grad, jnp.stack([key_grad, value_grad]))


def per_device(tokens, query_weight, key_weight, value_weight, output_grad, segments):
    tok_rows = tokens.shape[0]
    hop_count = HOPS
    margin = hop_count * tok_rows
    gathered = lax.all_gather(tokens, "head", axis=1, tiled=True)
    queries = jnp.dot(gathered, query_weight, preferred_element_type=jnp.float32).astype(
        jnp.bfloat16
    )
    keys_own = jnp.dot(gathered, key_weight, preferred_element_type=jnp.float32).astype(
        jnp.bfloat16
    )
    values_own = jnp.dot(gathered, value_weight, preferred_element_type=jnp.float32).astype(
        jnp.bfloat16
    )
    key_value = jnp.stack([keys_own, values_own])
    blocks = [key_value] * (hop_count + 1)
    for distance in range(1, hop_count + 1):
        blocks[hop_count - distance] = passed_along(key_value, "seq", distance)
    keys_all = jnp.concatenate(blocks, axis=1)
    position = lax.axis_index("seq")
    query_first = position * tok_rows
    seg_query = lax.dynamic_slice_in_dim(segments, query_first, tok_rows, 0)
    seg_padded = jnp.concatenate([jnp.full((margin,), -1, jnp.int32), segments], axis=0)
    seg_key = lax.dynamic_slice_in_dim(seg_padded, query_first, (hop_count + 1) * tok_rows, 0)
    query_grad, kv_grad = attend(
        queries, keys_all, output_grad, query_first, query_first - margin, seg_query, seg_key
    )
    pieces = [
        kv_grad[:, block * tok_rows : (block + 1) * tok_rows] for block in range(hop_count + 1)
    ]
    carried = pieces[hop_count]
    for distance in range(1, hop_count + 1):
        back = passed_along(pieces[hop_count - distance].astype(jnp.bfloat16), "seq", -distance)
        carried = carried + back.astype(jnp.float32)
    key_grad = carried[0].astype(jnp.bfloat16)
    value_grad = carried[1].astype(jnp.bfloat16)
    n_head = lax.axis_size("head")
    me = lax.axis_index("head")
    width = tokens.shape[1]

    def term(dest):
        start = dest * width
        part = contract_last(query_grad, lax.dynamic_slice_in_dim(query_weight, start, width, 0))
        part = part + contract_last(key_grad, lax.dynamic_slice_in_dim(key_weight, start, width, 0))
        part = part + contract_last(value_grad, lax.dynamic_slice_in_dim(value_weight, start, width, 0))
        return part.astype(jnp.bfloat16)

    token_sum = None
    for shift in range(n_head - 1, 0, -1):
        sent = term((me + shift) % n_head)
        pairs = [(i, (i + shift) % n_head) for i in range(n_head)]
        got = lax.ppermute(sent, "head", pairs).astype(jnp.float32)
        token_sum = got if token_sum is None else token_sum + got
    own = term(me).astype(jnp.float32)
    token_grad = (own if token_sum is None else token_sum + own).astype(jnp.bfloat16)
    proj_grads = jnp.concatenate([query_grad, key_grad, value_grad], axis=1)
    summed = lax.psum_scatter(
        contract_first(proj_grads, gathered).astype(jnp.bfloat16),
        "seq",
        scatter_dimension=1,
        tiled=True,
    ).astype(jnp.float32)
    summed = (summed * (tok_rows * lax.axis_size("seq")) ** (-0.5)).astype(jnp.bfloat16).T
    q_width = query_weight.shape[1]
    k_width = key_weight.shape[1]
    query_weight_grad = summed[:, :q_width]
    key_weight_grad = summed[:, q_width : q_width + k_width]
    value_weight_grad = summed[:, q_width + k_width :]
    return (token_grad, query_weight_grad, key_weight_grad, value_weight_grad)


def solution(mesh):
    in_specs = (
        P("seq", "head"),
        P(None, "head"),
        P(None, "head"),
        P(None, "head"),
        P("seq", "head"),
        P(),
    )
    out_specs = (P("seq", "head"), P("seq", "head"), P("seq", "head"), P("seq", "head"))
    return jax.shard_map(
        per_device, mesh=mesh, in_specs=in_specs, out_specs=out_specs, check_vma=False
    )
```

```python
import jax
import jax.numpy as jnp
from jax import lax
from jax.experimental import pallas as pl
from jax.experimental.pallas import tpu as pltpu
from jax.sharding import PartitionSpec as P

D = 5376
HEADS = 32
KV_HEADS = 16
HEAD_DIM = 128
WINDOW = 1024
HOPS = 2


neg_large = -1e30


def passed_along(x, axis, by):
    count = lax.axis_size(axis)
    pairs = [(i, i + by) for i in range(count) if 0 <= i + by < count]
    return lax.ppermute(x, axis, pairs)


def contract_last(left, right):
    return lax.dot_general(
        left, right, (((1,), (1,)), ((), ())), preferred_element_type=jnp.float32
    )


def contract_first(left, right):
    return lax.dot_general(
        left, right, (((0,), (0,)), ((), ())), preferred_element_type=jnp.float32
    )


def attention_kernel(mask_ref, q_ref, k_ref, v_ref, g_ref, qg_ref, kg_ref, vg_ref):
    score_scale = (D / HEADS) ** (-0.5)
    groups = q_ref.shape[1] // HEAD_DIM
    tok_rows = q_ref.shape[0]
    half = tok_rows // 2
    span = WINDOW + half
    kg_ref[...] = jnp.zeros(kg_ref.shape, jnp.float32)
    vg_ref[...] = jnp.zeros(vg_ref.shape, jnp.float32)
    for piece in range(2):
        rows = slice(piece * half, (piece + 1) * half)
        reach = slice(piece * half, piece * half + span)
        allowed = mask_ref[rows, reach] > 0.5
        keys = k_ref[0, reach, :]
        values = v_ref[0, reach, :]
        key_acc = jnp.zeros((span, HEAD_DIM), jnp.float32)
        value_acc = jnp.zeros((span, HEAD_DIM), jnp.float32)
        for group in range(groups):
            cols = slice(group * HEAD_DIM, (group + 1) * HEAD_DIM)
            queries = q_ref[rows, cols]
            grads = g_ref[rows, cols]
            scores = contract_last(queries, keys) * score_scale
            masked = jnp.where(allowed, scores, neg_large)
            row_max = jnp.max(masked, axis=-1, keepdims=True)
            expo = jnp.where(allowed, jnp.exp(masked - row_max), 0.0)
            probs = expo / jnp.sum(expo, axis=-1, keepdims=True)
            dprobs = contract_last(grads, values)
            center = jnp.sum(probs * dprobs, axis=-1, keepdims=True)
            dscores = (probs * (dprobs - center)).astype(jnp.bfloat16)
            probs_low = probs.astype(jnp.bfloat16)
            query_grad = jnp.dot(dscores, keys, preferred_element_type=jnp.float32) * score_scale
            qg_ref[rows, cols] = query_grad.astype(jnp.bfloat16)
            key_acc = key_acc + contract_first(dscores, queries)
            value_acc = value_acc + contract_first(probs_low, grads)
        kg_ref[reach, :] = kg_ref[reach, :] + key_acc * score_scale
        vg_ref[reach, :] = vg_ref[reach, :] + value_acc


def attend(queries, key_value, grads, query_first, key_first, seg_query, seg_key):
    tok_rows = queries.shape[0]
    key_rows = key_value.shape[1]
    groups = HEADS // KV_HEADS
    kv_local = key_value.shape[2] // HEAD_DIM
    query_pos = query_first + jnp.arange(tok_rows, dtype=jnp.int32)
    key_pos = key_first + jnp.arange(key_rows, dtype=jnp.int32)
    spacing = query_pos[:, None] - key_pos[None, :]
    allowed = (
        (key_pos >= 0)[None, :]
        & (spacing >= 0)
        & (spacing < WINDOW)
        & (seg_query[:, None] == seg_key[None, :])
    )
    assert key_rows == WINDOW + tok_rows and tok_rows % 256 == 0
    mask = allowed.astype(jnp.float32)
    q_spec = pl.BlockSpec((tok_rows, groups * HEAD_DIM), lambda h: (0, h))
    kv_out_spec = pl.BlockSpec((key_rows, HEAD_DIM), lambda h: (0, h))
    query_grad, key_grad, value_grad = pl.pallas_call(
        attention_kernel,
        grid=(kv_local,),
        in_specs=[
            pl.BlockSpec((tok_rows, key_rows), lambda h: (0, 0)),
            q_spec,
            pl.BlockSpec((1, key_rows, HEAD_DIM), lambda h: (0, 0, h)),
            pl.BlockSpec((1, key_rows, HEAD_DIM), lambda h: (1, 0, h)),
            q_spec,
        ],
        out_specs=[q_spec, kv_out_spec, kv_out_spec],
        out_shape=[
            jax.ShapeDtypeStruct(queries.shape, jnp.bfloat16),
            jax.ShapeDtypeStruct(key_value.shape[1:], jnp.float32),
            jax.ShapeDtypeStruct(key_value.shape[1:], jnp.float32),
        ],
        compiler_params=pltpu.CompilerParams(vmem_limit_bytes=56 * 1024 * 1024),
    )(mask, queries, key_value, key_value, grads)
    return (query_grad, jnp.stack([key_grad, value_grad]))


def per_device(tokens, query_weight, key_weight, value_weight, output_grad, segments):
    tok_rows = tokens.shape[0]
    hop_count = HOPS
    margin = hop_count * tok_rows
    gathered = lax.all_gather(tokens, "head", axis=1, tiled=True)
    queries = jnp.dot(gathered, query_weight, preferred_element_type=jnp.float32).astype(
        jnp.bfloat16
    )
    keys_own = jnp.dot(gathered, key_weight, preferred_element_type=jnp.float32).astype(
        jnp.bfloat16
    )
    values_own = jnp.dot(gathered, value_weight, preferred_element_type=jnp.float32).astype(
        jnp.bfloat16
    )
    key_value = jnp.stack([keys_own, values_own])
    blocks = [key_value] * (hop_count + 1)
    moving = key_value
    for distance in range(1, hop_count + 1):
        moving = passed_along(moving, "seq", 1)
        blocks[hop_count - distance] = moving
    keys_all = jnp.concatenate(blocks, axis=1)
    position = lax.axis_index("seq")
    query_first = position * tok_rows
    seg_query = lax.dynamic_slice_in_dim(segments, query_first, tok_rows, 0)
    seg_padded = jnp.concatenate([jnp.full((margin,), -1, jnp.int32), segments], axis=0)
    seg_key = lax.dynamic_slice_in_dim(seg_padded, query_first, (hop_count + 1) * tok_rows, 0)
    query_grad, kv_grad = attend(
        queries, keys_all, output_grad, query_first, query_first - margin, seg_query, seg_key
    )
    pieces = [
        kv_grad[:, block * tok_rows : (block + 1) * tok_rows] for block in range(hop_count + 1)
    ]
    carried = pieces[0]
    for distance in range(1, hop_count + 1):
        carried = pieces[distance] + passed_along(carried.astype(jnp.bfloat16), "seq", -1).astype(
            carried.dtype
        )
    key_grad = carried[0].astype(jnp.bfloat16)
    value_grad = carried[1].astype(jnp.bfloat16)
    n_head = lax.axis_size("head")
    me = lax.axis_index("head")
    width = tokens.shape[1]

    def term(dest):
        start = dest * width
        part = contract_last(query_grad, lax.dynamic_slice_in_dim(query_weight, start, width, 0))
        part = part + contract_last(key_grad, lax.dynamic_slice_in_dim(key_weight, start, width, 0))
        part = part + contract_last(value_grad, lax.dynamic_slice_in_dim(value_weight, start, width, 0))
        return part.astype(jnp.bfloat16)

    token_sum = None
    for shift in range(n_head - 1, 0, -1):
        sent = term((me + shift) % n_head)
        pairs = [(i, (i + shift) % n_head) for i in range(n_head)]
        got = lax.ppermute(sent, "head", pairs).astype(jnp.float32)
        token_sum = got if token_sum is None else token_sum + got
    own = term(me).astype(jnp.float32)
    token_grad = (own if token_sum is None else token_sum + own).astype(jnp.bfloat16)
    proj_grads = jnp.concatenate([query_grad, key_grad, value_grad], axis=1)
    summed = lax.psum_scatter(
        contract_first(proj_grads, gathered).astype(jnp.bfloat16),
        "seq",
        scatter_dimension=1,
        tiled=True,
    ).astype(jnp.float32)
    summed = (summed * (tok_rows * lax.axis_size("seq")) ** (-0.5)).astype(jnp.bfloat16).T
    q_width = query_weight.shape[1]
    k_width = key_weight.shape[1]
    query_weight_grad = summed[:, :q_width]
    key_weight_grad = summed[:, q_width : q_width + k_width]
    value_weight_grad = summed[:, q_width + k_width :]
    return (token_grad, query_weight_grad, key_weight_grad, value_weight_grad)


def solution(mesh):
    in_specs = (
        P("seq", "head"),
        P(None, "head"),
        P(None, "head"),
        P(None, "head"),
        P("seq", "head"),
        P(),
    )
    out_specs = (P("seq", "head"), P("seq", "head"), P("seq", "head"), P("seq", "head"))
    return jax.shard_map(
        per_device, mesh=mesh, in_specs=in_specs, out_specs=out_specs, check_vma=False
    )
```

```python
import jax
import jax.numpy as jnp
from jax import lax
from jax.experimental import pallas as pl
from jax.experimental.pallas import tpu as pltpu
from jax.sharding import PartitionSpec as P

D = 5376
HEADS = 32
KV_HEADS = 16
HEAD_DIM = 128
WINDOW = 1024
HOPS = 2


neg_large = -1e30


def passed_along(x, axis, by):
    count = lax.axis_size(axis)
    pairs = [(i, i + by) for i in range(count) if 0 <= i + by < count]
    return lax.ppermute(x, axis, pairs)


def contract_last(left, right):
    return lax.dot_general(
        left, right, (((1,), (1,)), ((), ())), preferred_element_type=jnp.float32
    )


def contract_first(left, right):
    return lax.dot_general(
        left, right, (((0,), (0,)), ((), ())), preferred_element_type=jnp.float32
    )


def attention_kernel(mask_ref, q_ref, k_ref, v_ref, g_ref, qg_ref, kg_ref, vg_ref):
    score_scale = (D / HEADS) ** (-0.5)
    groups = q_ref.shape[1] // HEAD_DIM
    tok_rows = q_ref.shape[0]
    half = tok_rows // 2
    span = WINDOW + half
    kg_ref[...] = jnp.zeros(kg_ref.shape, jnp.float32)
    vg_ref[...] = jnp.zeros(vg_ref.shape, jnp.float32)
    for piece in range(2):
        rows = slice(piece * half, (piece + 1) * half)
        reach = slice(piece * half, piece * half + span)
        allowed_one = mask_ref[rows, reach] > 0.5
        allowed = jnp.concatenate([allowed_one] * groups, axis=0)
        keys = k_ref[0, reach, :]
        values = v_ref[0, reach, :]
        col = [slice(group * HEAD_DIM, (group + 1) * HEAD_DIM) for group in range(groups)]
        queries = jnp.concatenate([q_ref[rows, c] for c in col], axis=0)
        grads = jnp.concatenate([g_ref[rows, c] for c in col], axis=0)
        scores = contract_last(queries, keys) * score_scale
        masked = jnp.where(allowed, scores, neg_large)
        row_max = jnp.max(masked, axis=-1, keepdims=True)
        expo = jnp.where(allowed, jnp.exp(masked - row_max), 0.0)
        probs = expo / jnp.sum(expo, axis=-1, keepdims=True)
        dprobs = contract_last(grads, values)
        center = jnp.sum(probs * dprobs, axis=-1, keepdims=True)
        dscores = (probs * (dprobs - center)).astype(jnp.bfloat16)
        probs_low = probs.astype(jnp.bfloat16)
        query_grad = jnp.dot(dscores, keys, preferred_element_type=jnp.float32) * score_scale
        query_grad = query_grad.astype(jnp.bfloat16)
        for group in range(groups):
            qg_ref[rows, col[group]] = query_grad[group * half : (group + 1) * half]
        kg_ref[reach, :] = kg_ref[reach, :] + contract_first(dscores, queries) * score_scale
        vg_ref[reach, :] = vg_ref[reach, :] + contract_first(probs_low, grads)


def attend(queries, key_value, grads, query_first, key_first, seg_query, seg_key):
    tok_rows = queries.shape[0]
    key_rows = key_value.shape[1]
    groups = HEADS // KV_HEADS
    kv_local = key_value.shape[2] // HEAD_DIM
    query_pos = query_first + jnp.arange(tok_rows, dtype=jnp.int32)
    key_pos = key_first + jnp.arange(key_rows, dtype=jnp.int32)
    spacing = query_pos[:, None] - key_pos[None, :]
    allowed = (
        (key_pos >= 0)[None, :]
        & (spacing >= 0)
        & (spacing < WINDOW)
        & (seg_query[:, None] == seg_key[None, :])
    )
    assert key_rows == WINDOW + tok_rows and tok_rows % 256 == 0
    mask = allowed.astype(jnp.float32)
    q_spec = pl.BlockSpec((tok_rows, groups * HEAD_DIM), lambda h: (0, h))
    kv_out_spec = pl.BlockSpec((key_rows, HEAD_DIM), lambda h: (0, h))
    query_grad, key_grad, value_grad = pl.pallas_call(
        attention_kernel,
        grid=(kv_local,),
        in_specs=[
            pl.BlockSpec((tok_rows, key_rows), lambda h: (0, 0)),
            q_spec,
            pl.BlockSpec((1, key_rows, HEAD_DIM), lambda h: (0, 0, h)),
            pl.BlockSpec((1, key_rows, HEAD_DIM), lambda h: (1, 0, h)),
            q_spec,
        ],
        out_specs=[q_spec, kv_out_spec, kv_out_spec],
        out_shape=[
            jax.ShapeDtypeStruct(queries.shape, jnp.bfloat16),
            jax.ShapeDtypeStruct(key_value.shape[1:], jnp.float32),
            jax.ShapeDtypeStruct(key_value.shape[1:], jnp.float32),
        ],
        compiler_params=pltpu.CompilerParams(vmem_limit_bytes=56 * 1024 * 1024),
    )(mask, queries, key_value, key_value, grads)
    return (query_grad, jnp.stack([key_grad, value_grad]))


def per_device(tokens, query_weight, key_weight, value_weight, output_grad, segments):
    tok_rows = tokens.shape[0]
    hop_count = HOPS
    margin = hop_count * tok_rows
    gathered = lax.all_gather(tokens, "head", axis=1, tiled=True)
    queries = jnp.dot(gathered, query_weight, preferred_element_type=jnp.float32).astype(
        jnp.bfloat16
    )
    keys_own = jnp.dot(gathered, key_weight, preferred_element_type=jnp.float32).astype(
        jnp.bfloat16
    )
    values_own = jnp.dot(gathered, value_weight, preferred_element_type=jnp.float32).astype(
        jnp.bfloat16
    )
    key_value = jnp.stack([keys_own, values_own])
    blocks = [key_value] * (hop_count + 1)
    moving = key_value
    for distance in range(1, hop_count + 1):
        moving = passed_along(moving, "seq", 1)
        blocks[hop_count - distance] = moving
    keys_all = jnp.concatenate(blocks, axis=1)
    position = lax.axis_index("seq")
    query_first = position * tok_rows
    seg_query = lax.dynamic_slice_in_dim(segments, query_first, tok_rows, 0)
    seg_padded = jnp.concatenate([jnp.full((margin,), -1, jnp.int32), segments], axis=0)
    seg_key = lax.dynamic_slice_in_dim(seg_padded, query_first, (hop_count + 1) * tok_rows, 0)
    query_grad, kv_grad = attend(
        queries, keys_all, output_grad, query_first, query_first - margin, seg_query, seg_key
    )
    pieces = [
        kv_grad[:, block * tok_rows : (block + 1) * tok_rows] for block in range(hop_count + 1)
    ]
    carried = pieces[0]
    for distance in range(1, hop_count + 1):
        carried = pieces[distance] + passed_along(carried.astype(jnp.bfloat16), "seq", -1).astype(
            carried.dtype
        )
    key_grad = carried[0].astype(jnp.bfloat16)
    value_grad = carried[1].astype(jnp.bfloat16)
    n_head = lax.axis_size("head")
    me = lax.axis_index("head")
    width = tokens.shape[1]

    def term(dest):
        start = dest * width
        part = contract_last(query_grad, lax.dynamic_slice_in_dim(query_weight, start, width, 0))
        part = part + contract_last(key_grad, lax.dynamic_slice_in_dim(key_weight, start, width, 0))
        part = part + contract_last(value_grad, lax.dynamic_slice_in_dim(value_weight, start, width, 0))
        return part.astype(jnp.bfloat16)

    token_sum = None
    for shift in range(n_head - 1, 0, -1):
        sent = term((me + shift) % n_head)
        pairs = [(i, (i + shift) % n_head) for i in range(n_head)]
        got = lax.ppermute(sent, "head", pairs).astype(jnp.float32)
        token_sum = got if token_sum is None else token_sum + got
    own = term(me).astype(jnp.float32)
    token_grad = (own if token_sum is None else token_sum + own).astype(jnp.bfloat16)
    proj_grads = jnp.concatenate([query_grad, key_grad, value_grad], axis=1)
    summed = lax.psum_scatter(
        contract_first(proj_grads, gathered).astype(jnp.bfloat16),
        "seq",
        scatter_dimension=1,
        tiled=True,
    ).astype(jnp.float32)
    summed = (summed * (tok_rows * lax.axis_size("seq")) ** (-0.5)).astype(jnp.bfloat16).T
    q_width = query_weight.shape[1]
    k_width = key_weight.shape[1]
    query_weight_grad = summed[:, :q_width]
    key_weight_grad = summed[:, q_width : q_width + k_width]
    value_weight_grad = summed[:, q_width + k_width :]
    return (token_grad, query_weight_grad, key_weight_grad, value_weight_grad)


def solution(mesh):
    in_specs = (
        P("seq", "head"),
        P(None, "head"),
        P(None, "head"),
        P(None, "head"),
        P("seq", "head"),
        P(),
    )
    out_specs = (P("seq", "head"), P("seq", "head"), P("seq", "head"), P("seq", "head"))
    return jax.shard_map(
        per_device, mesh=mesh, in_specs=in_specs, out_specs=out_specs, check_vma=False
    )
```

```python
import jax
import jax.numpy as jnp
from jax import lax
from jax.experimental import pallas as pl
from jax.experimental.pallas import tpu as pltpu
from jax.sharding import PartitionSpec as P

D = 5376
HEADS = 32
KV_HEADS = 16
HEAD_DIM = 128
WINDOW = 1024
HOPS = 2


neg_large = -1e30


def passed_along(x, axis, by):
    count = lax.axis_size(axis)
    pairs = [(i, i + by) for i in range(count) if 0 <= i + by < count]
    return lax.ppermute(x, axis, pairs)


def contract_last(left, right):
    return lax.dot_general(
        left, right, (((1,), (1,)), ((), ())), preferred_element_type=jnp.float32
    )


def contract_first(left, right):
    return lax.dot_general(
        left, right, (((0,), (0,)), ((), ())), preferred_element_type=jnp.float32
    )


def attention_kernel(mask_ref, q_ref, k_ref, v_ref, g_ref, qg_ref, kg_ref, vg_ref):
    score_scale = (D / HEADS) ** (-0.5)
    groups = q_ref.shape[1] // HEAD_DIM
    tok_rows = q_ref.shape[0]
    half = tok_rows // 2
    span = WINDOW + half
    kg_ref[...] = jnp.zeros(kg_ref.shape, jnp.float32)
    vg_ref[...] = jnp.zeros(vg_ref.shape, jnp.float32)
    for piece in range(2):
        rows = slice(piece * half, (piece + 1) * half)
        reach = slice(piece * half, piece * half + span)
        allowed = mask_ref[rows, reach] > 0.5
        keys = k_ref[0, reach, :]
        values = v_ref[0, reach, :]
        key_acc = jnp.zeros((span, HEAD_DIM), jnp.float32)
        value_acc = jnp.zeros((span, HEAD_DIM), jnp.float32)
        for group in range(groups):
            cols = slice(group * HEAD_DIM, (group + 1) * HEAD_DIM)
            queries = q_ref[rows, cols]
            grads = g_ref[rows, cols]
            scores = contract_last(queries, keys) * score_scale
            masked = jnp.where(allowed, scores, neg_large)
            row_max = jnp.max(masked, axis=-1, keepdims=True)
            expo = jnp.where(allowed, jnp.exp(masked - row_max), 0.0)
            probs = expo / jnp.sum(expo, axis=-1, keepdims=True)
            dprobs = contract_last(grads, values)
            center = jnp.sum(probs * dprobs, axis=-1, keepdims=True)
            dscores = (probs * (dprobs - center)).astype(jnp.bfloat16)
            probs_low = probs.astype(jnp.bfloat16)
            query_grad = jnp.dot(dscores, keys, preferred_element_type=jnp.float32) * score_scale
            qg_ref[rows, cols] = query_grad.astype(jnp.bfloat16)
            key_acc = key_acc + contract_first(dscores, queries)
            value_acc = value_acc + contract_first(probs_low, grads)
        kg_ref[reach, :] = kg_ref[reach, :] + key_acc * score_scale
        vg_ref[reach, :] = vg_ref[reach, :] + value_acc


def attend(queries, key_value, grads, query_first, key_first, seg_query, seg_key):
    tok_rows = queries.shape[0]
    key_rows = key_value.shape[1]
    groups = HEADS // KV_HEADS
    kv_local = key_value.shape[2] // HEAD_DIM
    query_pos = query_first + jnp.arange(tok_rows, dtype=jnp.int32)
    key_pos = key_first + jnp.arange(key_rows, dtype=jnp.int32)
    spacing = query_pos[:, None] - key_pos[None, :]
    allowed = (
        (key_pos >= 0)[None, :]
        & (spacing >= 0)
        & (spacing < WINDOW)
        & (seg_query[:, None] == seg_key[None, :])
    )
    assert key_rows == WINDOW + tok_rows and tok_rows % 256 == 0
    mask = allowed.astype(jnp.float32)
    q_spec = pl.BlockSpec((tok_rows, groups * HEAD_DIM), lambda h: (0, h))
    kv_out_spec = pl.BlockSpec((key_rows, HEAD_DIM), lambda h: (0, h))
    query_grad, key_grad, value_grad = pl.pallas_call(
        attention_kernel,
        grid=(kv_local,),
        in_specs=[
            pl.BlockSpec((tok_rows, key_rows), lambda h: (0, 0)),
            q_spec,
            pl.BlockSpec((1, key_rows, HEAD_DIM), lambda h: (0, 0, h)),
            pl.BlockSpec((1, key_rows, HEAD_DIM), lambda h: (1, 0, h)),
            q_spec,
        ],
        out_specs=[q_spec, kv_out_spec, kv_out_spec],
        out_shape=[
            jax.ShapeDtypeStruct(queries.shape, jnp.bfloat16),
            jax.ShapeDtypeStruct(key_value.shape[1:], jnp.float32),
            jax.ShapeDtypeStruct(key_value.shape[1:], jnp.float32),
        ],
        compiler_params=pltpu.CompilerParams(vmem_limit_bytes=56 * 1024 * 1024),
    )(mask, queries, key_value, key_value, grads)
    return (query_grad, jnp.stack([key_grad, value_grad]))


def per_device(tokens, query_weight, key_weight, value_weight, output_grad, segments):
    tok_rows = tokens.shape[0]
    hop_count = HOPS
    margin = hop_count * tok_rows
    gathered = lax.all_gather(tokens, "head", axis=1, tiled=True)
    queries = jnp.dot(gathered, query_weight, preferred_element_type=jnp.float32).astype(
        jnp.bfloat16
    )
    keys_own = jnp.dot(gathered, key_weight, preferred_element_type=jnp.float32).astype(
        jnp.bfloat16
    )
    values_own = jnp.dot(gathered, value_weight, preferred_element_type=jnp.float32).astype(
        jnp.bfloat16
    )
    key_value = jnp.stack([keys_own, values_own])
    blocks = [key_value] * (hop_count + 1)
    moving = key_value
    for distance in range(1, hop_count + 1):
        if distance > 1:
            moving, queries = lax.optimization_barrier((moving, queries))
        moving = passed_along(moving, "seq", 1)
        blocks[hop_count - distance] = moving
    keys_all = jnp.concatenate(blocks, axis=1)
    position = lax.axis_index("seq")
    query_first = position * tok_rows
    seg_query = lax.dynamic_slice_in_dim(segments, query_first, tok_rows, 0)
    seg_padded = jnp.concatenate([jnp.full((margin,), -1, jnp.int32), segments], axis=0)
    seg_key = lax.dynamic_slice_in_dim(seg_padded, query_first, (hop_count + 1) * tok_rows, 0)
    query_grad, kv_grad = attend(
        queries, keys_all, output_grad, query_first, query_first - margin, seg_query, seg_key
    )
    pieces = [
        kv_grad[:, block * tok_rows : (block + 1) * tok_rows] for block in range(hop_count + 1)
    ]
    carried = pieces[0]
    for distance in range(1, hop_count + 1):
        carried = pieces[distance] + passed_along(carried.astype(jnp.bfloat16), "seq", -1).astype(
            carried.dtype
        )
    key_grad = carried[0].astype(jnp.bfloat16)
    value_grad = carried[1].astype(jnp.bfloat16)
    n_head = lax.axis_size("head")
    me = lax.axis_index("head")
    width = tokens.shape[1]

    def term(dest):
        start = dest * width
        part = contract_last(query_grad, lax.dynamic_slice_in_dim(query_weight, start, width, 0))
        part = part + contract_last(key_grad, lax.dynamic_slice_in_dim(key_weight, start, width, 0))
        part = part + contract_last(value_grad, lax.dynamic_slice_in_dim(value_weight, start, width, 0))
        return part.astype(jnp.bfloat16)

    token_sum = None
    for shift in range(n_head - 1, 0, -1):
        sent = term((me + shift) % n_head)
        pairs = [(i, (i + shift) % n_head) for i in range(n_head)]
        got = lax.ppermute(sent, "head", pairs).astype(jnp.float32)
        token_sum = got if token_sum is None else token_sum + got
    own = term(me).astype(jnp.float32)
    token_grad = (own if token_sum is None else token_sum + own).astype(jnp.bfloat16)
    proj_grads = jnp.concatenate([query_grad, key_grad, value_grad], axis=1)
    summed = lax.psum_scatter(
        contract_first(proj_grads, gathered).astype(jnp.bfloat16),
        "seq",
        scatter_dimension=1,
        tiled=True,
    ).astype(jnp.float32)
    summed = (summed * (tok_rows * lax.axis_size("seq")) ** (-0.5)).astype(jnp.bfloat16).T
    q_width = query_weight.shape[1]
    k_width = key_weight.shape[1]
    query_weight_grad = summed[:, :q_width]
    key_weight_grad = summed[:, q_width : q_width + k_width]
    value_weight_grad = summed[:, q_width + k_width :]
    return (token_grad, query_weight_grad, key_weight_grad, value_weight_grad)


def solution(mesh):
    in_specs = (
        P("seq", "head"),
        P(None, "head"),
        P(None, "head"),
        P(None, "head"),
        P("seq", "head"),
        P(),
    )
    out_specs = (P("seq", "head"), P("seq", "head"), P("seq", "head"), P("seq", "head"))
    return jax.shard_map(
        per_device, mesh=mesh, in_specs=in_specs, out_specs=out_specs, check_vma=False
    )
```

```python
import jax
import jax.numpy as jnp
from jax import lax
from jax.experimental import pallas as pl
from jax.experimental.pallas import tpu as pltpu
from jax.sharding import PartitionSpec as P

D = 5376
HEADS = 32
KV_HEADS = 16
HEAD_DIM = 128
WINDOW = 1024
HOPS = 2


neg_large = -1e30


def passed_along(x, axis, by):
    count = lax.axis_size(axis)
    pairs = [(i, i + by) for i in range(count) if 0 <= i + by < count]
    return lax.ppermute(x, axis, pairs)


def contract_last(left, right):
    return lax.dot_general(
        left, right, (((1,), (1,)), ((), ())), preferred_element_type=jnp.float32
    )


def contract_first(left, right):
    return lax.dot_general(
        left, right, (((0,), (0,)), ((), ())), preferred_element_type=jnp.float32
    )


def attention_kernel(mask_ref, q_ref, k_ref, v_ref, g_ref, qg_ref, kg_ref, vg_ref):
    score_scale = (D / HEADS) ** (-0.5)
    groups = q_ref.shape[1] // HEAD_DIM
    tok_rows = q_ref.shape[0]
    half = tok_rows // 2
    span = WINDOW + half
    kg_ref[...] = jnp.zeros(kg_ref.shape, jnp.float32)
    vg_ref[...] = jnp.zeros(vg_ref.shape, jnp.float32)
    for piece in range(2):
        rows = slice(piece * half, (piece + 1) * half)
        reach = slice(piece * half, piece * half + span)
        allowed = mask_ref[rows, reach] > 0.5
        keys = k_ref[0, reach, :]
        values = v_ref[0, reach, :]
        key_acc = jnp.zeros((span, HEAD_DIM), jnp.float32)
        value_acc = jnp.zeros((span, HEAD_DIM), jnp.float32)
        for group in range(groups):
            cols = slice(group * HEAD_DIM, (group + 1) * HEAD_DIM)
            queries = q_ref[rows, cols]
            grads = g_ref[rows, cols]
            scores = contract_last(queries, keys) * score_scale
            masked = jnp.where(allowed, scores, neg_large)
            row_max = jnp.max(masked, axis=-1, keepdims=True)
            expo = jnp.exp(masked - row_max)
            probs = expo * (1.0 / jnp.sum(expo, axis=-1, keepdims=True))
            dprobs = contract_last(grads, values)
            center = jnp.sum(probs * dprobs, axis=-1, keepdims=True)
            dscores = (probs * (dprobs - center)).astype(jnp.bfloat16)
            probs_low = probs.astype(jnp.bfloat16)
            query_grad = jnp.dot(dscores, keys, preferred_element_type=jnp.float32) * score_scale
            qg_ref[rows, cols] = query_grad.astype(jnp.bfloat16)
            key_acc = key_acc + contract_first(dscores, queries)
            value_acc = value_acc + contract_first(probs_low, grads)
        kg_ref[reach, :] = kg_ref[reach, :] + key_acc * score_scale
        vg_ref[reach, :] = vg_ref[reach, :] + value_acc


def attend(queries, key_value, grads, query_first, key_first, seg_query, seg_key):
    tok_rows = queries.shape[0]
    key_rows = key_value.shape[1]
    groups = HEADS // KV_HEADS
    kv_local = key_value.shape[2] // HEAD_DIM
    query_pos = query_first + jnp.arange(tok_rows, dtype=jnp.int32)
    key_pos = key_first + jnp.arange(key_rows, dtype=jnp.int32)
    spacing = query_pos[:, None] - key_pos[None, :]
    allowed = (
        (key_pos >= 0)[None, :]
        & (spacing >= 0)
        & (spacing < WINDOW)
        & (seg_query[:, None] == seg_key[None, :])
    )
    assert key_rows == WINDOW + tok_rows and tok_rows % 256 == 0
    mask = allowed.astype(jnp.float32)
    q_spec = pl.BlockSpec((tok_rows, groups * HEAD_DIM), lambda h: (0, h))
    kv_out_spec = pl.BlockSpec((key_rows, HEAD_DIM), lambda h: (0, h))
    query_grad, key_grad, value_grad = pl.pallas_call(
        attention_kernel,
        grid=(kv_local,),
        in_specs=[
            pl.BlockSpec((tok_rows, key_rows), lambda h: (0, 0)),
            q_spec,
            pl.BlockSpec((1, key_rows, HEAD_DIM), lambda h: (0, 0, h)),
            pl.BlockSpec((1, key_rows, HEAD_DIM), lambda h: (1, 0, h)),
            q_spec,
        ],
        out_specs=[q_spec, kv_out_spec, kv_out_spec],
        out_shape=[
            jax.ShapeDtypeStruct(queries.shape, jnp.bfloat16),
            jax.ShapeDtypeStruct(key_value.shape[1:], jnp.float32),
            jax.ShapeDtypeStruct(key_value.shape[1:], jnp.float32),
        ],
        compiler_params=pltpu.CompilerParams(vmem_limit_bytes=56 * 1024 * 1024),
    )(mask, queries, key_value, key_value, grads)
    return (query_grad, jnp.stack([key_grad, value_grad]))


def per_device(tokens, query_weight, key_weight, value_weight, output_grad, segments):
    tok_rows = tokens.shape[0]
    hop_count = HOPS
    margin = hop_count * tok_rows
    gathered = lax.all_gather(tokens, "head", axis=1, tiled=True)
    queries = jnp.dot(gathered, query_weight, preferred_element_type=jnp.float32).astype(
        jnp.bfloat16
    )
    keys_own = jnp.dot(gathered, key_weight, preferred_element_type=jnp.float32).astype(
        jnp.bfloat16
    )
    values_own = jnp.dot(gathered, value_weight, preferred_element_type=jnp.float32).astype(
        jnp.bfloat16
    )
    key_value = jnp.stack([keys_own, values_own])
    blocks = [key_value] * (hop_count + 1)
    moving = key_value
    for distance in range(1, hop_count + 1):
        moving = passed_along(moving, "seq", 1)
        blocks[hop_count - distance] = moving
    keys_all = jnp.concatenate(blocks, axis=1)
    position = lax.axis_index("seq")
    query_first = position * tok_rows
    seg_query = lax.dynamic_slice_in_dim(segments, query_first, tok_rows, 0)
    seg_padded = jnp.concatenate([jnp.full((margin,), -1, jnp.int32), segments], axis=0)
    seg_key = lax.dynamic_slice_in_dim(seg_padded, query_first, (hop_count + 1) * tok_rows, 0)
    query_grad, kv_grad = attend(
        queries, keys_all, output_grad, query_first, query_first - margin, seg_query, seg_key
    )
    pieces = [
        kv_grad[:, block * tok_rows : (block + 1) * tok_rows] for block in range(hop_count + 1)
    ]
    carried = pieces[0]
    for distance in range(1, hop_count + 1):
        carried = pieces[distance] + passed_along(carried.astype(jnp.bfloat16), "seq", -1).astype(
            carried.dtype
        )
    key_grad = carried[0].astype(jnp.bfloat16)
    value_grad = carried[1].astype(jnp.bfloat16)
    n_head = lax.axis_size("head")
    me = lax.axis_index("head")
    width = tokens.shape[1]

    def term(dest):
        start = dest * width
        part = contract_last(query_grad, lax.dynamic_slice_in_dim(query_weight, start, width, 0))
        part = part + contract_last(key_grad, lax.dynamic_slice_in_dim(key_weight, start, width, 0))
        part = part + contract_last(value_grad, lax.dynamic_slice_in_dim(value_weight, start, width, 0))
        return part.astype(jnp.bfloat16)

    token_sum = None
    for shift in range(n_head - 1, 0, -1):
        sent = term((me + shift) % n_head)
        pairs = [(i, (i + shift) % n_head) for i in range(n_head)]
        got = lax.ppermute(sent, "head", pairs).astype(jnp.float32)
        token_sum = got if token_sum is None else token_sum + got
    own = term(me).astype(jnp.float32)
    token_grad = (own if token_sum is None else token_sum + own).astype(jnp.bfloat16)
    proj_grads = jnp.concatenate([query_grad, key_grad, value_grad], axis=1)
    summed = lax.psum_scatter(
        contract_first(proj_grads, gathered).astype(jnp.bfloat16),
        "seq",
        scatter_dimension=1,
        tiled=True,
    ).astype(jnp.float32)
    summed = (summed * (tok_rows * lax.axis_size("seq")) ** (-0.5)).astype(jnp.bfloat16).T
    q_width = query_weight.shape[1]
    k_width = key_weight.shape[1]
    query_weight_grad = summed[:, :q_width]
    key_weight_grad = summed[:, q_width : q_width + k_width]
    value_weight_grad = summed[:, q_width + k_width :]
    return (token_grad, query_weight_grad, key_weight_grad, value_weight_grad)


def solution(mesh):
    in_specs = (
        P("seq", "head"),
        P(None, "head"),
        P(None, "head"),
        P(None, "head"),
        P("seq", "head"),
        P(),
    )
    out_specs = (P("seq", "head"), P("seq", "head"), P("seq", "head"), P("seq", "head"))
    return jax.shard_map(
        per_device, mesh=mesh, in_specs=in_specs, out_specs=out_specs, check_vma=False
    )
```

```python
import jax
import jax.numpy as jnp
from jax import lax
from jax.experimental import pallas as pl
from jax.experimental.pallas import tpu as pltpu
from jax.sharding import PartitionSpec as P

D = 5376
HEADS = 32
KV_HEADS = 16
HEAD_DIM = 128
WINDOW = 1024
HOPS = 2


neg_large = -1e30


def passed_along(x, axis, by):
    count = lax.axis_size(axis)
    pairs = [(i, i + by) for i in range(count) if 0 <= i + by < count]
    return lax.ppermute(x, axis, pairs)


def contract_last(left, right):
    return lax.dot_general(
        left, right, (((1,), (1,)), ((), ())), preferred_element_type=jnp.float32
    )


def contract_first(left, right):
    return lax.dot_general(
        left, right, (((0,), (0,)), ((), ())), preferred_element_type=jnp.float32
    )


def attention_kernel(mask_ref, q_ref, k_ref, v_ref, g_ref, qg_ref, kg_ref, vg_ref):
    score_scale = (D / HEADS) ** (-0.5)
    groups = q_ref.shape[1] // HEAD_DIM
    tok_rows = q_ref.shape[0]
    half = tok_rows // 2
    span = WINDOW + half
    kg_ref[...] = jnp.zeros(kg_ref.shape, jnp.float32)
    vg_ref[...] = jnp.zeros(vg_ref.shape, jnp.float32)
    for piece in range(2):
        rows = slice(piece * half, (piece + 1) * half)
        reach = slice(piece * half, piece * half + span)
        allowed = mask_ref[rows, reach] > 0.5
        keys = k_ref[0, reach, :]
        values = v_ref[0, reach, :]
        key_acc = jnp.zeros((span, HEAD_DIM), jnp.float32)
        value_acc = jnp.zeros((span, HEAD_DIM), jnp.float32)
        for group in range(groups):
            cols = slice(group * HEAD_DIM, (group + 1) * HEAD_DIM)
            queries = q_ref[rows, cols]
            grads = g_ref[rows, cols]
            scores = contract_last(queries, keys) * score_scale
            masked = jnp.where(allowed, scores, neg_large)
            row_max = jnp.max(masked, axis=-1, keepdims=True)
            expo = jnp.exp(masked - row_max)
            probs = expo * (1.0 / jnp.sum(expo, axis=-1, keepdims=True))
            dprobs = contract_last(grads, values)
            center = jnp.sum(probs * dprobs, axis=-1, keepdims=True)
            dscores = (probs * (dprobs - center)).astype(jnp.bfloat16)
            probs_low = probs.astype(jnp.bfloat16)
            query_grad = jnp.dot(dscores, keys, preferred_element_type=jnp.float32) * score_scale
            qg_ref[rows, cols] = query_grad.astype(jnp.bfloat16)
            key_acc = key_acc + contract_first(dscores, queries)
            value_acc = value_acc + contract_first(probs_low, grads)
        kg_ref[reach, :] = kg_ref[reach, :] + key_acc * score_scale
        vg_ref[reach, :] = vg_ref[reach, :] + value_acc


def attend(queries, key_value, grads, query_first, key_first, seg_query, seg_key):
    tok_rows = queries.shape[0]
    key_rows = key_value.shape[1]
    groups = HEADS // KV_HEADS
    kv_local = key_value.shape[2] // HEAD_DIM
    query_pos = query_first + jnp.arange(tok_rows, dtype=jnp.int32)
    key_pos = key_first + jnp.arange(key_rows, dtype=jnp.int32)
    spacing = query_pos[:, None] - key_pos[None, :]
    allowed = (
        (key_pos >= 0)[None, :]
        & (spacing >= 0)
        & (spacing < WINDOW)
        & (seg_query[:, None] == seg_key[None, :])
    )
    assert key_rows == WINDOW + tok_rows and tok_rows % 256 == 0
    mask = allowed.astype(jnp.bfloat16)
    q_spec = pl.BlockSpec((tok_rows, groups * HEAD_DIM), lambda h: (0, h))
    kv_out_spec = pl.BlockSpec((key_rows, HEAD_DIM), lambda h: (0, h))
    query_grad, key_grad, value_grad = pl.pallas_call(
        attention_kernel,
        grid=(kv_local,),
        in_specs=[
            pl.BlockSpec((tok_rows, key_rows), lambda h: (0, 0)),
            q_spec,
            pl.BlockSpec((1, key_rows, HEAD_DIM), lambda h: (0, 0, h)),
            pl.BlockSpec((1, key_rows, HEAD_DIM), lambda h: (1, 0, h)),
            q_spec,
        ],
        out_specs=[q_spec, kv_out_spec, kv_out_spec],
        out_shape=[
            jax.ShapeDtypeStruct(queries.shape, jnp.bfloat16),
            jax.ShapeDtypeStruct(key_value.shape[1:], jnp.float32),
            jax.ShapeDtypeStruct(key_value.shape[1:], jnp.float32),
        ],
        compiler_params=pltpu.CompilerParams(vmem_limit_bytes=56 * 1024 * 1024),
    )(mask, queries, key_value, key_value, grads)
    return (query_grad, jnp.stack([key_grad, value_grad]))


def per_device(tokens, query_weight, key_weight, value_weight, output_grad, segments):
    tok_rows = tokens.shape[0]
    hop_count = HOPS
    margin = hop_count * tok_rows
    gathered = lax.all_gather(tokens, "head", axis=1, tiled=True)
    queries = jnp.dot(gathered, query_weight, preferred_element_type=jnp.float32).astype(
        jnp.bfloat16
    )
    keys_own = jnp.dot(gathered, key_weight, preferred_element_type=jnp.float32).astype(
        jnp.bfloat16
    )
    values_own = jnp.dot(gathered, value_weight, preferred_element_type=jnp.float32).astype(
        jnp.bfloat16
    )
    key_value = jnp.stack([keys_own, values_own])
    blocks = [key_value] * (hop_count + 1)
    moving = key_value
    for distance in range(1, hop_count + 1):
        moving = passed_along(moving, "seq", 1)
        blocks[hop_count - distance] = moving
    keys_all = jnp.concatenate(blocks, axis=1)
    position = lax.axis_index("seq")
    query_first = position * tok_rows
    seg_query = lax.dynamic_slice_in_dim(segments, query_first, tok_rows, 0)
    seg_padded = jnp.concatenate([jnp.full((margin,), -1, jnp.int32), segments], axis=0)
    seg_key = lax.dynamic_slice_in_dim(seg_padded, query_first, (hop_count + 1) * tok_rows, 0)
    query_grad, kv_grad = attend(
        queries, keys_all, output_grad, query_first, query_first - margin, seg_query, seg_key
    )
    pieces = [
        kv_grad[:, block * tok_rows : (block + 1) * tok_rows] for block in range(hop_count + 1)
    ]
    carried = pieces[0]
    for distance in range(1, hop_count + 1):
        carried = pieces[distance] + passed_along(carried.astype(jnp.bfloat16), "seq", -1).astype(
            carried.dtype
        )
    key_grad = carried[0].astype(jnp.bfloat16)
    value_grad = carried[1].astype(jnp.bfloat16)
    n_head = lax.axis_size("head")
    me = lax.axis_index("head")
    width = tokens.shape[1]

    def term(dest):
        start = dest * width
        part = contract_last(query_grad, lax.dynamic_slice_in_dim(query_weight, start, width, 0))
        part = part + contract_last(key_grad, lax.dynamic_slice_in_dim(key_weight, start, width, 0))
        part = part + contract_last(value_grad, lax.dynamic_slice_in_dim(value_weight, start, width, 0))
        return part.astype(jnp.bfloat16)

    token_sum = None
    for shift in range(n_head - 1, 0, -1):
        sent = term((me + shift) % n_head)
        pairs = [(i, (i + shift) % n_head) for i in range(n_head)]
        got = lax.ppermute(sent, "head", pairs).astype(jnp.float32)
        token_sum = got if token_sum is None else token_sum + got
    own = term(me).astype(jnp.float32)
    token_grad = (own if token_sum is None else token_sum + own).astype(jnp.bfloat16)
    proj_grads = jnp.concatenate([query_grad, key_grad, value_grad], axis=1)
    summed = lax.psum_scatter(
        contract_first(proj_grads, gathered).astype(jnp.bfloat16),
        "seq",
        scatter_dimension=1,
        tiled=True,
    ).astype(jnp.float32)
    summed = (summed * (tok_rows * lax.axis_size("seq")) ** (-0.5)).astype(jnp.bfloat16).T
    q_width = query_weight.shape[1]
    k_width = key_weight.shape[1]
    query_weight_grad = summed[:, :q_width]
    key_weight_grad = summed[:, q_width : q_width + k_width]
    value_weight_grad = summed[:, q_width + k_width :]
    return (token_grad, query_weight_grad, key_weight_grad, value_weight_grad)


def solution(mesh):
    in_specs = (
        P("seq", "head"),
        P(None, "head"),
        P(None, "head"),
        P(None, "head"),
        P("seq", "head"),
        P(),
    )
    out_specs = (P("seq", "head"), P("seq", "head"), P("seq", "head"), P("seq", "head"))
    return jax.shard_map(
        per_device, mesh=mesh, in_specs=in_specs, out_specs=out_specs, check_vma=False
    )
```
